512 devices in a mesh: slab: 64 (over y, z_lo, core), plane: 8 (over x, z_hi).
Axes of the slice: x: 4, y: 4, z: 16 (z_hi: 2, z_lo: 8; z = z_hi * 8 + z_lo), core: 2. Of those that a mesh axis runs over, the one named last changes fastest.
Arguments:
- rock_state: float32 [2, 128, 64, 512], P(None, 'slab', 'plane'), may hold values from -6 to 6
- rock_source: float32 [2, 128, 64, 512], P(None, 'slab', 'plane'), may hold values from -6 to 6
- transmissibility: bfloat16 [3, 128, 64, 512], P(None, 'slab', 'plane'), may hold values from 0.039794922 to 0.29882812
- cell_inverse: bfloat16 [4, 128, 64, 512], P(None, 'slab', 'plane'), may hold values from -0.06 to 0.3
- fracture_state: float32 [2, 524288], P(None, ('slab', 'plane')), may hold values from -6 to 6
- fracture_source: float32 [2, 524288], P(None, ('slab', 'plane')), may hold values from -6 to 6
- fracture_coupling: bfloat16 [4096, 3, 128, 128], P(('slab', 'plane')), may hold values from -0.25 to 0.25
- fracture_inverse: bfloat16 [4096, 128, 128], P(('slab', 'plane')), may hold values from -0.044194174 to 0.3941942
- fracture_neighbours: int32 [4096, 3], P(('slab', 'plane')), may hold values from 0 to 4095, as said below
- contact_cell: int32 [64, 512, 128], P('slab', 'plane'), may hold values from 0 to 8191
- contact_segment: int32 [64, 512, 128], P('slab', 'plane'), may hold values from 0 to 1023
- contact_weight: float32 [64, 512, 128], P('slab', 'plane'), may hold values from 0.3 to 1.5
- contact_count: int32 [64, 512], P('slab', 'plane'), may hold values from 32 to 128, as said below
Outputs:
- rock_final: float32 [2, 128, 64, 512], P(None, 'slab', 'plane')
- fracture_final: float32 [2, 524288], P(None, ('slab', 'plane'))
The draws below stay inside these ranges and needn't reach their ends.
Inputs may be any that keep to these rules, and one draw needn't show every extreme that they name: `contact_count`: live contact slots from one rock device to one fracture part of the same plane index; for every plane index some fracture part receives 128 live slots from every rock slab. `fracture_neighbours`: a block's neighbours are other blocks of its own part or of the parts one step away along slab with the same plane index.
All inputs are finite; a program needn't handle non-finite values.
Results may differ from the reference program's by a relative error of at most 0.0033.
Values may be sent and summed in bfloat16 or wider, within the bound.
No kernel may reach another device: no remote copies, remote signals or barrier semaphores. Data moves between devices by JAX's collectives and lax.ppermute only.
A program may use at most 64 MiB of HBM per device.

```python
import math
import jax
import jax.numpy as jnp
from jax import lax

CZ = 2
CX = 8
NY = 512
FB_DEV = 8
NB = 128
NNB = 3
CAP = 128
ITERS = 3
NZ = 128
NX = 64
BLOCKS = 4096
SEGS = 524288
N_SLAB = 64
N_PLANE = 8


def draw_cell_inverse(key, part):
    key_diag, key_off = jax.random.split(jax.random.fold_in(key, 11))
    shape = (2, NZ, NX, NY)
    diagonal = jnp.exp(jax.random.uniform(key_diag, shape, jnp.float32, math.log(0.1), math.log(0.295)))
    coupling = jax.random.uniform(key_off, shape, jnp.float32, -0.059, 0.059)
    return jnp.stack([diagonal[0], coupling[0], coupling[1], diagonal[1]]).astype(jnp.bfloat16)


def draw_fracture_inverse(key, part):
    key_diag, key_off = jax.random.split(jax.random.fold_in(key, 23))
    diagonal = jnp.exp(jax.random.uniform(key_diag, (BLOCKS, NB), jnp.float32, math.log(0.15), math.log(0.35)))
    spread = jnp.clip(jax.random.normal(key_off, (BLOCKS, NB, NB), jnp.float32), -4.0, 4.0) * 0.12
    matrix = spread / math.sqrt(NB) + diagonal[:, :, None] * jnp.eye(NB, dtype=jnp.float32)[None]
    return matrix.astype(jnp.bfloat16)


def draw_fracture_neighbours(key, part):
    key_off, key_pick = jax.random.split(jax.random.fold_in(key, 37))
    block_index = jnp.arange(BLOCKS, dtype=jnp.int32)
    owner_part = block_index // FB_DEV
    local_index = block_index % FB_DEV
    slab_index = owner_part // N_PLANE
    offset = jax.random.randint(key_off, (BLOCKS, NNB), -1, 2, jnp.int32)
    target = slab_index[:, None] + offset
    offset = jnp.where((target >= 0) & (target < N_SLAB), offset, 0)
    chosen = jax.random.randint(key_pick, (BLOCKS, NNB), 0, FB_DEV, jnp.int32)
    chosen = jnp.where((offset == 0) & (chosen == local_index[:, None]), (chosen + 1) % FB_DEV, chosen)
    return ((owner_part[:, None] + offset * N_PLANE) * FB_DEV + chosen).astype(jnp.int32)


def draw_contact_count(key, part):
    key_base, key_busy, key_force = jax.random.split(jax.random.fold_in(key, 53), 3)
    base_count = jax.random.randint(key_base, (N_SLAB, N_PLANE * N_SLAB), CAP // 4, CAP // 2 + 1, jnp.int32)
    busy_part = jax.random.randint(key_busy, (N_PLANE, N_SLAB), 0, 8, jnp.int32) == 0
    forced = jax.random.randint(key_force, (N_PLANE, 1), 0, N_SLAB, jnp.int32)
    busy_part = busy_part | (jnp.arange(N_SLAB, dtype=jnp.int32)[None, :] == forced)
    return jnp.where(busy_part.reshape(1, -1), CAP, base_count).astype(jnp.int32)


def touch_ends(result, own_key, least, largest):
    longest = result.shape.index(max(result.shape))
    spots = []
    for shift in (0, 1):
        where = [jax.random.randint(jax.random.fold_in(own_key, axis), (), 0, length) for axis, length in enumerate(result.shape)]
        where[longest] = (where[longest] + shift) % result.shape[longest]
        spots.append(tuple(where))
    return result.at[spots[0]].set(least).at[spots[1]].set(largest)


def steps_of(stream_key, extent, pieces, low, largest):
    loudness, own = 1.0, jax.random.fold_in(stream_key, 6)
    for axis_at, parts in pieces:
        draws = jnp.exp(jax.random.uniform(jax.random.fold_in(own, axis_at), (parts,), jnp.float32, low / len(pieces), largest / len(pieces)))
        loudness = loudness * jnp.repeat(draws, extent[axis_at] // parts).reshape([-1 if axis == axis_at else 1 for axis in range(len(extent))])
    return loudness


def scatter_about(stream_key, dims, deviation, limit, shards=(), held_as=jnp.bfloat16):
    result = deviation * jax.random.normal(stream_key, dims, jnp.float32)
    if shards:
        result = result * steps_of(stream_key, dims, shards, -0.22, 0.18)
    return jnp.clip(result, -limit, limit).astype(held_as)


def setup_inputs(seed: int = 0) -> dict:
    seeds = jax.random.split(jax.random.key(seed), 14)
    return {
        "rock_state": scatter_about(seeds[0], (2, NZ, NX, NY), 1.0, 6.0, ((1, 64), (2, 8)), jnp.float32),
        "rock_source": scatter_about(seeds[1], (2, NZ, NX, NY), 1.0, 6.0, ((1, 64), (2, 8)), jnp.float32),
        "transmissibility": jnp.clip(jnp.exp(math.log(0.29882812) - 2.0161293 * jax.random.uniform(seeds[2], (3, NZ, NX, NY), jnp.float32) ** steps_of(seeds[2], (3, NZ, NX, NY), ((1, 64), (2, 8)), -0.2, 0.2)), 0.039794922, 0.29882812).astype(jnp.bfloat16),
        "cell_inverse": draw_cell_inverse(jax.random.fold_in(seeds[13], 71), 0),
        "fracture_state": scatter_about(seeds[4], (2, SEGS), 1.0, 6.0, ((1, 512),), jnp.float32),
        "fracture_source": scatter_about(seeds[5], (2, SEGS), 1.0, 6.0, ((1, 512),), jnp.float32),
        "fracture_coupling": scatter_about(seeds[6], (BLOCKS, NNB, NB, NB), (4 * NB) ** -0.5, 0.25, ((0, 512),)),
        "fracture_inverse": draw_fracture_inverse(jax.random.fold_in(seeds[13], 71), 0),
        "fracture_neighbours": draw_fracture_neighbours(jax.random.fold_in(seeds[13], 71), 0),
        "contact_cell": touch_ends(jax.random.randint(seeds[9], (N_SLAB, N_PLANE * N_SLAB, CAP), 0, CZ * CX * NY), jax.random.fold_in(seeds[9], 1), 0, (CZ * CX * NY) - 1).astype(jnp.int32),
        "contact_segment": touch_ends(jax.random.randint(seeds[10], (N_SLAB, N_PLANE * N_SLAB, CAP), 0, FB_DEV * NB), jax.random.fold_in(seeds[10], 1), 0, (FB_DEV * NB) - 1).astype(jnp.int32),
        "contact_weight": jnp.clip(jnp.exp(math.log(1.5) - 1.60943787 * jax.random.uniform(seeds[11], (N_SLAB, N_PLANE * N_SLAB, CAP), jnp.float32) ** steps_of(seeds[11], (N_SLAB, N_PLANE * N_SLAB, CAP), ((0, 64), (1, 8)), -0.2, 0.2)), 0.3, 1.5),
        "contact_count": draw_contact_count(jax.random.fold_in(seeds[13], 71), 0),
    }


def couple_group(pair):
    matrices, states = pair
    return jnp.einsum("bkij,bkfj->bfi", matrices.astype(jnp.float32), states.astype(jnp.float32))


def invert_group(pair):
    matrices, states = pair
    return jnp.einsum("bij,bfj->bfi", matrices.astype(jnp.float32), states.astype(jnp.float32))


def reference(rock_state, rock_source, transmissibility, cell_inverse, fracture_state, fracture_source, fracture_coupling, fracture_inverse, fracture_neighbours, contact_cell, contact_segment, contact_weight, contact_count):
    source_slab = jnp.arange(N_SLAB, dtype=jnp.int32)[:, None, None]
    column = jnp.arange(N_PLANE * N_SLAB, dtype=jnp.int32)[None, :, None]
    plane_index = column // N_SLAB
    target_slab = column % N_SLAB
    layer_z = contact_cell // (CX * NY)
    layer_x = (contact_cell // NY) % CX
    layer_y = contact_cell % NY
    global_cell = (((source_slab * CZ + layer_z) * NX + plane_index * CX + layer_x) * NY + layer_y).reshape(-1).astype(jnp.int32)
    global_segment = ((target_slab * N_PLANE + plane_index) * FB_DEV * NB + contact_segment).reshape(-1).astype(jnp.int32)
    slot_index = jnp.arange(CAP, dtype=jnp.int32)[None, None, :]
    slot_weight = jnp.where(slot_index < contact_count[:, :, None], contact_weight, jnp.zeros_like(contact_weight)).reshape(-1)
    coef = transmissibility.astype(jnp.float32)
    coef_next = jnp.stack([
        jnp.pad(coef[0, 1:], ((0, 1), (0, 0), (0, 0))),
        jnp.pad(coef[1, :, 1:], ((0, 0), (0, 1), (0, 0))),
        jnp.pad(coef[2, :, :, 1:], ((0, 0), (0, 0), (0, 1)))])
    inverse = cell_inverse.astype(jnp.float32)
    groups = BLOCKS // FB_DEV
    coupling_groups = fracture_coupling.reshape(groups, FB_DEV, NNB, NB, NB)
    inverse_groups = fracture_inverse.reshape(groups, FB_DEV, NB, NB)
    cell_total = NZ * NX * NY
    source_blocks = fracture_source.reshape(2, BLOCKS, NB).transpose(1, 0, 2)
    rock_now = rock_state
    fracture_now = fracture_state
    for sweep_index in range(ITERS):
        rock_flat = rock_now.reshape(2, -1)
        leak_fracture = jax.ops.segment_sum((slot_weight * rock_flat[:, global_cell]).T, global_segment, num_segments=SEGS).T
        leak_rock = jax.ops.segment_sum((slot_weight * fracture_now[:, global_segment]).T, global_cell, num_segments=cell_total).T.reshape(rock_now.shape)
        fracture_low = fracture_now.astype(jnp.bfloat16).reshape(2, BLOCKS, NB).transpose(1, 0, 2)
        gathered = fracture_low[fracture_neighbours]
        coupled = lax.map(couple_group, (coupling_groups, gathered.reshape(groups, FB_DEV, NNB, 2, NB))).reshape(BLOCKS, 2, NB)
        leak_blocks = leak_fracture.reshape(2, BLOCKS, NB).transpose(1, 0, 2)
        fracture_rhs = (source_blocks + leak_blocks - coupled).astype(jnp.bfloat16)
        fracture_next = lax.map(invert_group, (inverse_groups, fracture_rhs.reshape(groups, FB_DEV, 2, NB)))
        fracture_next = fracture_next.reshape(BLOCKS, 2, NB).transpose(1, 0, 2).reshape(2, -1)
        padded = jnp.pad(rock_now, ((0, 0), (1, 1), (1, 1), (1, 1)))
        near_sum = coef[0] * padded[:, :-2, 1:-1, 1:-1] + coef[1] * padded[:, 1:-1, :-2, 1:-1] + coef[2] * padded[:, 1:-1, 1:-1, :-2]
        near_sum = near_sum + coef_next[0] * padded[:, 2:, 1:-1, 1:-1] + coef_next[1] * padded[:, 1:-1, 2:, 1:-1] + coef_next[2] * padded[:, 1:-1, 1:-1, 2:]
        rock_rhs = rock_source + near_sum + leak_rock
        rock_now = jnp.stack([inverse[0] * rock_rhs[0] + inverse[1] * rock_rhs[1], inverse[2] * rock_rhs[0] + inverse[3] * rock_rhs[1]])
        fracture_now = fracture_next
    return rock_now, fracture_now
```

```python
import jax
import jax.numpy as jnp
from jax import lax
from jax.sharding import PartitionSpec as P


ITERS = 3


def shifted(value, axis, steps):
    count = lax.axis_size(axis)
    first, last = (max(0, -steps), min(count, count - steps))
    return lax.ppermute(value, axis, [(source, source + steps) for source in range(first, last)])


def split_bf16(value):
    high = lax.reduce_precision(value, exponent_bits=8, mantissa_bits=7)
    return high.astype(jnp.bfloat16), (value - high).astype(jnp.bfloat16)


def pick_values(row_onehot, col_mask, table):
    fields = table.shape[0]
    high, low = split_bf16(table)
    parts = jnp.concatenate([high, low], 0)
    by_row = jnp.einsum("kc,grc->gkr", col_mask, parts, preferred_element_type=jnp.float32)
    picked = jnp.sum(by_row * row_onehot.astype(jnp.float32)[None], axis=-1)
    return picked[:fields] + picked[fields:]


def place_values(row_onehot, col_mask, values):
    fields = values.shape[0]
    high, low = split_bf16(values)
    parts = jnp.concatenate([high, low], 0)
    spread = parts[:, :, None] * row_onehot[None]
    placed = jnp.einsum("gkr,kc->grc", spread, col_mask, preferred_element_type=jnp.float32)
    return placed[:fields] + placed[fields:]


def shards(
    rock_state,
    rock_source,
    transmissibility,
    cell_inverse,
    fracture_state,
    fracture_source,
    fracture_coupling,
    fracture_inverse,
    fracture_neighbours,
    contact_cell,
    contact_segment,
    contact_weight,
    contact_count,
):
    plane_count = lax.axis_size("plane")
    slab_count = lax.axis_size("slab")
    blocks = fracture_coupling.shape[0]
    segment_width = fracture_coupling.shape[-1]
    cell_table = contact_cell[0]
    slot_shape = cell_table.shape
    slot_index = lax.broadcasted_iota(jnp.int32, slot_shape, 1)
    slot_weight = jnp.where(slot_index < contact_count[0][:, None], contact_weight[0], 0.0)
    slot_weight_flat = slot_weight.reshape(-1)
    arrived_segment = lax.all_to_all(
        contact_segment[0], "slab", split_axis=0, concat_axis=0, tiled=True
    )
    my_part = lax.axis_index("slab") * plane_count + lax.axis_index("plane")
    owner_part = fracture_neighbours // blocks
    position = ((owner_part - my_part) // plane_count + 1) * blocks + fracture_neighbours % blocks
    rim_onehot = (
        position[:, :, None] == lax.broadcasted_iota(jnp.int32, (1, 1, 3 * blocks), 2)
    ).astype(jnp.bfloat16)
    cell_total = rock_state[0].size
    cell_rows = cell_total // 128
    cell_flat = cell_table.reshape(-1)
    cell_row_onehot = (
        (cell_flat // 128)[:, None] == lax.broadcasted_iota(jnp.int32, (1, cell_rows), 1)
    ).astype(jnp.bfloat16)
    cell_col_mask = (
        (cell_flat % 128)[:, None] == lax.broadcasted_iota(jnp.int32, (1, 128), 1)
    ).astype(jnp.bfloat16)
    segment_flat = arrived_segment.reshape(-1)
    segment_row_onehot = (
        (segment_flat // segment_width)[:, None] == lax.broadcasted_iota(jnp.int32, (1, blocks), 1)
    ).astype(jnp.bfloat16)
    segment_col_mask = (
        (segment_flat % segment_width)[:, None]
        == lax.broadcasted_iota(jnp.int32, (1, segment_width), 1)
    ).astype(jnp.bfloat16)
    coef_z = transmissibility[0]
    coef_x = transmissibility[1]
    coef_y = transmissibility[2]
    layer_above = shifted(transmissibility[0, :1], "slab", -1)
    layer_beside = shifted(transmissibility[1, :, :1], "plane", -1)
    upper_z = jnp.concatenate([coef_z[1:], layer_above], 0)
    upper_x = jnp.concatenate([coef_x[:, 1:], layer_beside], 1)
    upper_y = jnp.pad(coef_y[..., 1:], ((0, 0), (0, 0), (0, 1)))
    forward_slab = [(i, i + 1) for i in range(slab_count - 1)]
    backward_slab = [(i + 1, i) for i in range(slab_count - 1)]
    forward_plane = [(i, i + 1) for i in range(plane_count - 1)]
    backward_plane = [(i + 1, i) for i in range(plane_count - 1)]
    rock_now = rock_state
    fracture_now = fracture_state
    source_blocks = fracture_source.reshape(2, blocks, segment_width)
    for _ in range(ITERS):
        rock_table = rock_now.reshape(2, cell_rows, 128)
        rock_picked = pick_values(cell_row_onehot, cell_col_mask, rock_table)
        send_rock = slot_weight_flat[None] * rock_picked
        fracture_table = fracture_now.reshape(2, blocks, segment_width)
        send_fracture = pick_values(segment_row_onehot, segment_col_mask, fracture_table)
        send = jnp.concatenate([send_rock, send_fracture], 0).reshape((4,) + slot_shape)
        got = lax.all_to_all(
            send.transpose(1, 0, 2), "slab", split_axis=0, concat_axis=0, tiled=True
        ).transpose(1, 0, 2)
        got_rock = got[:2].reshape(2, -1)
        got_fracture = got[2:].reshape(2, -1)
        fracture_low = fracture_now.astype(jnp.bfloat16).reshape(2, blocks, segment_width)
        fracture_wide = fracture_low.astype(jnp.float32).reshape(2, -1, rock_now.shape[-1])
        from_below = lax.ppermute(
            jnp.concatenate([rock_now[:, -1], fracture_wide], 1), "slab", forward_slab
        )
        from_above = lax.ppermute(
            jnp.concatenate([rock_now[:, 0], fracture_wide], 1), "slab", backward_slab
        )
        from_left = lax.ppermute(rock_now[:, :, -1], "plane", forward_plane)
        from_right = lax.ppermute(rock_now[:, :, 0], "plane", backward_plane)
        layer_rows = rock_now.shape[2]
        rock_below = from_below[:, None, :layer_rows]
        rock_above = from_above[:, None, :layer_rows]
        fracture_prev = from_below[:, layer_rows:].reshape(fracture_low.shape).astype(jnp.bfloat16)
        fracture_next_part = from_above[:, layer_rows:].reshape(
            fracture_low.shape
        ).astype(jnp.bfloat16)
        fracture_padded = jnp.concatenate([fracture_prev, fracture_low, fracture_next_part], 1)
        gathered = jnp.einsum(
            "bkq,fqj->fbkj", rim_onehot, fracture_padded, preferred_element_type=jnp.float32
        ).astype(jnp.bfloat16)
        coupled = jnp.einsum(
            "bkij,fbkj->fbi", fracture_coupling, gathered, preferred_element_type=jnp.float32
        )
        fracture_part = lax.optimization_barrier(source_blocks - coupled)
        below_z = jnp.concatenate([rock_below, rock_now[:, :-1]], 1)
        above_z = jnp.concatenate([rock_now[:, 1:], rock_above], 1)
        below_x = jnp.concatenate([from_left[:, :, None], rock_now[:, :, :-1]], 2)
        above_x = jnp.concatenate([rock_now[:, :, 1:], from_right[:, :, None]], 2)
        below_y = jnp.pad(rock_now[..., :-1], ((0, 0), (0, 0), (0, 0), (1, 0)))
        above_y = jnp.pad(rock_now[..., 1:], ((0, 0), (0, 0), (0, 0), (0, 1)))
        total = coef_z * below_z + upper_z * above_z
        total = total + coef_x * below_x + upper_x * above_x
        total = total + coef_y * below_y + upper_y * above_y
        rock_part = lax.optimization_barrier(rock_source + total)
        leak_fracture = place_values(segment_row_onehot, segment_col_mask, got_rock)
        leak_rock = place_values(
            cell_row_onehot, cell_col_mask, slot_weight_flat[None] * got_fracture
        ).reshape(rock_now.shape)
        fracture_rhs = (fracture_part + leak_fracture).astype(jnp.bfloat16)
        fracture_next = jnp.einsum(
            "bij,fbj->fbi", fracture_inverse, fracture_rhs, preferred_element_type=jnp.float32
        ).reshape(2, -1)
        rock_rhs = rock_part + leak_rock
        rock_now = jnp.stack(
            [
                cell_inverse[0] * rock_rhs[0] + cell_inverse[1] * rock_rhs[1],
                cell_inverse[2] * rock_rhs[0] + cell_inverse[3] * rock_rhs[1],
            ]
        )
        fracture_now = fracture_next
    return (rock_now, fracture_now)


def solution(mesh):
    return jax.shard_map(
        shards,
        mesh=mesh,
        in_specs=(
            P(None, "slab", "plane", None),
            P(None, "slab", "plane", None),
            P(None, "slab", "plane", None),
            P(None, "slab", "plane", None),
            P(None, ("slab", "plane")),
            P(None, ("slab", "plane")),
            P(("slab", "plane"), None, None, None),
            P(("slab", "plane"), None, None),
            P(("slab", "plane"), None),
            P("slab", "plane", None),
            P("slab", "plane", None),
            P("slab", "plane", None),
            P("slab", "plane"),
        ),
        out_specs=(P(None, "slab", "plane", None), P(None, ("slab", "plane"))),
        check_vma=False,
    )
```

```python
import jax
import jax.numpy as jnp
from jax import lax
from jax.sharding import PartitionSpec as P


ITERS = 3


def shifted(value, axis, steps):
    count = lax.axis_size(axis)
    first, last = (max(0, -steps), min(count, count - steps))
    return lax.ppermute(value, axis, [(source, source + steps) for source in range(first, last)])


def split_bf16(value):
    high = lax.reduce_precision(value, exponent_bits=8, mantissa_bits=7)
    return high.astype(jnp.bfloat16), (value - high).astype(jnp.bfloat16)


def pick_values(row_onehot, col_mask, table):
    fields = table.shape[0]
    high, low = split_bf16(table)
    parts = jnp.concatenate([high, low], 0)
    by_row = jnp.einsum("kc,grc->gkr", col_mask, parts, preferred_element_type=jnp.float32)
    picked = jnp.sum(by_row * row_onehot.astype(jnp.float32)[None], axis=-1)
    return picked[:fields] + picked[fields:]


def place_values(row_onehot, col_mask, values):
    fields = values.shape[0]
    high, low = split_bf16(values)
    parts = jnp.concatenate([high, low], 0)
    spread = parts[:, :, None] * row_onehot[None]
    placed = jnp.einsum("gkr,kc->grc", spread, col_mask, preferred_element_type=jnp.float32)
    return placed[:fields] + placed[fields:]


def shards(
    rock_state,
    rock_source,
    transmissibility,
    cell_inverse,
    fracture_state,
    fracture_source,
    fracture_coupling,
    fracture_inverse,
    fracture_neighbours,
    contact_cell,
    contact_segment,
    contact_weight,
    contact_count,
):
    plane_count = lax.axis_size("plane")
    slab_count = lax.axis_size("slab")
    blocks = fracture_coupling.shape[0]
    segment_width = fracture_coupling.shape[-1]
    cell_table = contact_cell[0]
    slot_shape = cell_table.shape
    slot_index = lax.broadcasted_iota(jnp.int32, slot_shape, 1)
    slot_weight = jnp.where(slot_index < contact_count[0][:, None], contact_weight[0], 0.0)
    slot_weight_flat = slot_weight.reshape(-1)
    arrived_segment = lax.all_to_all(
        contact_segment[0], "slab", split_axis=0, concat_axis=0, tiled=True
    )
    my_part = lax.axis_index("slab") * plane_count + lax.axis_index("plane")
    owner_part = fracture_neighbours // blocks
    position = ((owner_part - my_part) // plane_count + 1) * blocks + fracture_neighbours % blocks
    rim_onehot = (
        position[:, :, None] == lax.broadcasted_iota(jnp.int32, (1, 1, 3 * blocks), 2)
    ).astype(jnp.bfloat16)
    cell_total = rock_state[0].size
    cell_rows = cell_total // 128
    cell_flat = cell_table.reshape(-1)
    cell_row_onehot = (
        (cell_flat // 128)[:, None] == lax.broadcasted_iota(jnp.int32, (1, cell_rows), 1)
    ).astype(jnp.bfloat16)
    cell_col_mask = (
        (cell_flat % 128)[:, None] == lax.broadcasted_iota(jnp.int32, (1, 128), 1)
    ).astype(jnp.bfloat16)
    segment_flat = arrived_segment.reshape(-1)
    segment_row_onehot = (
        (segment_flat // segment_width)[:, None] == lax.broadcasted_iota(jnp.int32, (1, blocks), 1)
    ).astype(jnp.bfloat16)
    segment_col_mask = (
        (segment_flat % segment_width)[:, None]
        == lax.broadcasted_iota(jnp.int32, (1, segment_width), 1)
    ).astype(jnp.bfloat16)
    coef_z = transmissibility[0]
    coef_x = transmissibility[1]
    coef_y = transmissibility[2]
    layer_above = shifted(transmissibility[0, :1], "slab", -1)
    layer_beside = shifted(transmissibility[1, :, :1], "plane", -1)
    upper_z = jnp.concatenate([coef_z[1:], layer_above], 0)
    upper_x = jnp.concatenate([coef_x[:, 1:], layer_beside], 1)
    upper_y = jnp.pad(coef_y[..., 1:], ((0, 0), (0, 0), (0, 1)))
    forward_slab = [(i, i + 1) for i in range(slab_count - 1)]
    backward_slab = [(i + 1, i) for i in range(slab_count - 1)]
    rock_now = rock_state
    fracture_now = fracture_state
    source_blocks = fracture_source.reshape(2, blocks, segment_width)
    for _ in range(ITERS):
        rock_table = rock_now.reshape(2, cell_rows, 128)
        rock_picked = pick_values(cell_row_onehot, cell_col_mask, rock_table)
        send_rock = slot_weight_flat[None] * rock_picked
        fracture_table = fracture_now.reshape(2, blocks, segment_width)
        send_fracture = pick_values(segment_row_onehot, segment_col_mask, fracture_table)
        send = jnp.concatenate([send_rock, send_fracture], 0).reshape((4,) + slot_shape)
        got = lax.all_to_all(
            send.transpose(1, 0, 2), "slab", split_axis=0, concat_axis=0, tiled=True
        ).transpose(1, 0, 2)
        got_rock = got[:2].reshape(2, -1)
        got_fracture = got[2:].reshape(2, -1)
        fracture_low = fracture_now.astype(jnp.bfloat16).reshape(2, blocks, segment_width)
        fracture_wide = fracture_low.astype(jnp.float32).reshape(2, -1, rock_now.shape[-1])
        from_below = lax.ppermute(
            jnp.concatenate([rock_now[:, -1], fracture_wide], 1), "slab", forward_slab
        )
        from_above = lax.ppermute(
            jnp.concatenate([rock_now[:, 0], fracture_wide], 1), "slab", backward_slab
        )
        own_rims = jnp.stack([rock_now[:, :, 0], rock_now[:, :, -1]])
        slot = lax.broadcasted_iota(jnp.int32, (plane_count, 1, 1, 1, 1), 0)
        rims = lax.psum(jnp.where(slot == lax.axis_index("plane"), own_rims[None], 0.0), "plane")
        layer_rows = rock_now.shape[2]
        plane = lax.axis_index("plane")
        left_rim = lax.dynamic_index_in_dim(rims, jnp.maximum(plane - 1, 0), 0, False)[1]
        right_rim = lax.dynamic_index_in_dim(
            rims, jnp.minimum(plane + 1, plane_count - 1), 0, False
        )[0]
        from_left = jnp.where(plane > 0, left_rim, 0.0)
        from_right = jnp.where(plane < plane_count - 1, right_rim, 0.0)
        rock_below = from_below[:, None, :layer_rows]
        rock_above = from_above[:, None, :layer_rows]
        fracture_prev = from_below[:, layer_rows:].reshape(fracture_low.shape).astype(jnp.bfloat16)
        fracture_next_part = from_above[:, layer_rows:].reshape(
            fracture_low.shape
        ).astype(jnp.bfloat16)
        fracture_padded = jnp.concatenate([fracture_prev, fracture_low, fracture_next_part], 1)
        gathered = jnp.einsum(
            "bkq,fqj->fbkj", rim_onehot, fracture_padded, preferred_element_type=jnp.float32
        ).astype(jnp.bfloat16)
        coupled = jnp.einsum(
            "bkij,fbkj->fbi", fracture_coupling, gathered, preferred_element_type=jnp.float32
        )
        fracture_part = lax.optimization_barrier(source_blocks - coupled)
        below_z = jnp.concatenate([rock_below, rock_now[:, :-1]], 1)
        above_z = jnp.concatenate([rock_now[:, 1:], rock_above], 1)
        below_x = jnp.concatenate([from_left[:, :, None], rock_now[:, :, :-1]], 2)
        above_x = jnp.concatenate([rock_now[:, :, 1:], from_right[:, :, None]], 2)
        below_y = jnp.pad(rock_now[..., :-1], ((0, 0), (0, 0), (0, 0), (1, 0)))
        above_y = jnp.pad(rock_now[..., 1:], ((0, 0), (0, 0), (0, 0), (0, 1)))
        total = coef_z * below_z + upper_z * above_z
        total = total + coef_x * below_x + upper_x * above_x
        total = total + coef_y * below_y + upper_y * above_y
        rock_part = lax.optimization_barrier(rock_source + total)
        leak_fracture = place_values(segment_row_onehot, segment_col_mask, got_rock)
        leak_rock = place_values(
            cell_row_onehot, cell_col_mask, slot_weight_flat[None] * got_fracture
        ).reshape(rock_now.shape)
        fracture_rhs = (fracture_part + leak_fracture).astype(jnp.bfloat16)
        fracture_next = jnp.einsum(
            "bij,fbj->fbi", fracture_inverse, fracture_rhs, preferred_element_type=jnp.float32
        ).reshape(2, -1)
        rock_rhs = rock_part + leak_rock
        rock_now = jnp.stack(
            [
                cell_inverse[0] * rock_rhs[0] + cell_inverse[1] * rock_rhs[1],
                cell_inverse[2] * rock_rhs[0] + cell_inverse[3] * rock_rhs[1],
            ]
        )
        fracture_now = fracture_next
    return (rock_now, fracture_now)


def solution(mesh):
    return jax.shard_map(
        shards,
        mesh=mesh,
        in_specs=(
            P(None, "slab", "plane", None),
            P(None, "slab", "plane", None),
            P(None, "slab", "plane", None),
            P(None, "slab", "plane", None),
            P(None, ("slab", "plane")),
            P(None, ("slab", "plane")),
            P(("slab", "plane"), None, None, None),
            P(("slab", "plane"), None, None),
            P(("slab", "plane"), None),
            P("slab", "plane", None),
            P("slab", "plane", None),
            P("slab", "plane", None),
            P("slab", "plane"),
        ),
        out_specs=(P(None, "slab", "plane", None), P(None, ("slab", "plane"))),
        check_vma=False,
    )
```

```python
import jax
import jax.numpy as jnp
from jax import lax
from jax.sharding import PartitionSpec as P

from jax.experimental import pallas as pl
from jax.experimental.pallas import tpu as pltpu


ITERS = 3
INTERPRET = False


def shifted(value, axis, steps):
    count = lax.axis_size(axis)
    first, last = (max(0, -steps), min(count, count - steps))
    return lax.ppermute(value, axis, [(source, source + steps) for source in range(first, last)])


def split_bf16(value):
    high = lax.reduce_precision(value, exponent_bits=8, mantissa_bits=7)
    return high.astype(jnp.bfloat16), (value - high).astype(jnp.bfloat16)


def pick_values(row_onehot, col_mask, table):
    fields = table.shape[0]
    high, low = split_bf16(table)
    parts = jnp.concatenate([high, low], 0)
    by_row = jnp.einsum("kc,grc->gkr", col_mask, parts, preferred_element_type=jnp.float32)
    picked = jnp.sum(by_row * row_onehot.astype(jnp.float32)[None], axis=-1)
    return picked[:fields] + picked[fields:]


def place_values(row_onehot, col_mask, values):
    fields = values.shape[0]
    high, low = split_bf16(values)
    parts = jnp.concatenate([high, low], 0)
    spread = parts[:, :, None] * row_onehot[None]
    placed = jnp.einsum("gkr,kc->grc", spread, col_mask, preferred_element_type=jnp.float32)
    return placed[:fields] + placed[fields:]


def rock_kernel(
    rock_ref, source_ref, leak_ref, below_ref, above_ref, left_ref, right_ref, coef_ref, inv_ref,
    out_ref, low_ref, high_ref, first_ref, last_ref,
):
    depth, rows, lanes = rock_ref.shape[1:]
    row = lax.broadcasted_iota(jnp.int32, (rows, lanes), 0)
    lane = lax.broadcasted_iota(jnp.int32, (rows, lanes), 1)
    for z in range(depth):
        coef = [coef_ref[d, z].astype(jnp.float32) for d in range(6)]
        rhs = []
        for f in range(2):
            here = rock_ref[f, z]
            down = below_ref[f] if z == 0 else rock_ref[f, z - 1]
            up = above_ref[f] if z == depth - 1 else rock_ref[f, z + 1]
            west = jnp.where(row == 0, left_ref[f, z][None, :], pltpu.roll(here, 1, 0))
            east = jnp.where(row == rows - 1, right_ref[f, z][None, :], pltpu.roll(here, rows - 1, 0))
            south = jnp.where(lane == 0, 0.0, pltpu.roll(here, 1, 1))
            north = jnp.where(lane == lanes - 1, 0.0, pltpu.roll(here, lanes - 1, 1))
            total = coef[0] * down + coef[1] * up + coef[2] * west + coef[3] * east
            total = total + coef[4] * south + coef[5] * north
            rhs.append(source_ref[f, z] + total + leak_ref[f, z])
        inv = [inv_ref[i, z].astype(jnp.float32) for i in range(4)]
        for f in range(2):
            value = inv[2 * f] * rhs[0] + inv[2 * f + 1] * rhs[1]
            out_ref[f, z] = value
            first_ref[f, z] = value[0]
            last_ref[f, z] = value[rows - 1]
            if z == 0:
                low_ref[f] = value
            if z == depth - 1:
                high_ref[f] = value


def rock_step(rock, source, leak, below, above, left, right, coef, inverse):
    fields, depth, rows, lanes = rock.shape
    vmem = pl.BlockSpec(memory_space=pltpu.VMEM)
    return pl.pallas_call(
        rock_kernel,
        out_shape=(
            jax.ShapeDtypeStruct(rock.shape, jnp.float32),
            jax.ShapeDtypeStruct((fields, rows, lanes), jnp.float32),
            jax.ShapeDtypeStruct((fields, rows, lanes), jnp.float32),
            jax.ShapeDtypeStruct((fields, depth, lanes), jnp.float32),
            jax.ShapeDtypeStruct((fields, depth, lanes), jnp.float32),
        ),
        in_specs=[vmem] * 9,
        out_specs=(vmem,) * 5,
        cost_estimate=pl.CostEstimate(
            flops=40 * rock.size, transcendentals=0, bytes_accessed=20 * rock.size
        ),
        interpret=INTERPRET,
    )(rock, source, leak, below, above, left, right, coef, inverse)


def shards(
    rock_state,
    rock_source,
    transmissibility,
    cell_inverse,
    fracture_state,
    fracture_source,
    fracture_coupling,
    fracture_inverse,
    fracture_neighbours,
    contact_cell,
    contact_segment,
    contact_weight,
    contact_count,
):
    plane_count = lax.axis_size("plane")
    slab_count = lax.axis_size("slab")
    blocks = fracture_coupling.shape[0]
    segment_width = fracture_coupling.shape[-1]
    cell_table = contact_cell[0]
    slot_shape = cell_table.shape
    slot_index = lax.broadcasted_iota(jnp.int32, slot_shape, 1)
    slot_weight = jnp.where(slot_index < contact_count[0][:, None], contact_weight[0], 0.0)
    slot_weight_flat = slot_weight.reshape(-1)
    arrived_segment = lax.all_to_all(
        contact_segment[0], "slab", split_axis=0, concat_axis=0, tiled=True
    )
    my_part = lax.axis_index("slab") * plane_count + lax.axis_index("plane")
    owner_part = fracture_neighbours // blocks
    position = ((owner_part - my_part) // plane_count + 1) * blocks + fracture_neighbours % blocks
    rim_onehot = (
        position[:, :, None] == lax.broadcasted_iota(jnp.int32, (1, 1, 3 * blocks), 2)
    ).astype(jnp.bfloat16)
    cell_total = rock_state[0].size
    cell_rows = cell_total // 128
    cell_flat = cell_table.reshape(-1)
    cell_row_onehot = (
        (cell_flat // 128)[:, None] == lax.broadcasted_iota(jnp.int32, (1, cell_rows), 1)
    ).astype(jnp.bfloat16)
    cell_col_mask = (
        (cell_flat % 128)[:, None] == lax.broadcasted_iota(jnp.int32, (1, 128), 1)
    ).astype(jnp.bfloat16)
    segment_flat = arrived_segment.reshape(-1)
    segment_row_onehot = (
        (segment_flat // segment_width)[:, None] == lax.broadcasted_iota(jnp.int32, (1, blocks), 1)
    ).astype(jnp.bfloat16)
    segment_col_mask = (
        (segment_flat % segment_width)[:, None]
        == lax.broadcasted_iota(jnp.int32, (1, segment_width), 1)
    ).astype(jnp.bfloat16)
    coef_z = transmissibility[0]
    coef_x = transmissibility[1]
    coef_y = transmissibility[2]
    layer_above = shifted(transmissibility[0, :1], "slab", -1)
    layer_beside = shifted(transmissibility[1, :, :1], "plane", -1)
    upper_z = jnp.concatenate([coef_z[1:], layer_above], 0)
    upper_x = jnp.concatenate([coef_x[:, 1:], layer_beside], 1)
    upper_y = jnp.pad(coef_y[..., 1:], ((0, 0), (0, 0), (0, 1)))
    forward_slab = [(i, i + 1) for i in range(slab_count - 1)]
    backward_slab = [(i + 1, i) for i in range(slab_count - 1)]
    forward_plane = [(i, i + 1) for i in range(plane_count - 1)]
    backward_plane = [(i + 1, i) for i in range(plane_count - 1)]
    coef_all = jnp.stack([coef_z, upper_z, coef_x, upper_x, coef_y, upper_y])
    rock_now = rock_state
    rock_low, rock_high = rock_now[:, 0], rock_now[:, -1]
    rock_first, rock_last = rock_now[:, :, 0], rock_now[:, :, -1]
    fracture_now = fracture_state
    source_blocks = fracture_source.reshape(2, blocks, segment_width)
    layer_rows = rock_now.shape[2]
    for _ in range(ITERS):
        rock_table = rock_now.reshape(2, cell_rows, 128)
        rock_picked = pick_values(cell_row_onehot, cell_col_mask, rock_table)
        send_rock = slot_weight_flat[None] * rock_picked
        fracture_table = fracture_now.reshape(2, blocks, segment_width)
        send_fracture = pick_values(segment_row_onehot, segment_col_mask, fracture_table)
        send = jnp.concatenate([send_rock, send_fracture], 0).reshape((4,) + slot_shape)
        got = lax.all_to_all(
            send.transpose(1, 0, 2), "slab", split_axis=0, concat_axis=0, tiled=True
        ).transpose(1, 0, 2)
        got_rock = got[:2].reshape(2, -1)
        got_fracture = got[2:].reshape(2, -1)
        fracture_low = fracture_now.astype(jnp.bfloat16).reshape(2, blocks, segment_width)
        fracture_wide = fracture_low.astype(jnp.float32).reshape(2, -1, rock_now.shape[-1])
        from_below = lax.ppermute(
            jnp.concatenate([rock_high, fracture_wide], 1), "slab", forward_slab
        )
        from_above = lax.ppermute(
            jnp.concatenate([rock_low, fracture_wide], 1), "slab", backward_slab
        )
        from_left = lax.ppermute(rock_last, "plane", forward_plane)
        from_right = lax.ppermute(rock_first, "plane", backward_plane)
        fracture_prev = from_below[:, layer_rows:].reshape(fracture_low.shape).astype(jnp.bfloat16)
        fracture_next_part = from_above[:, layer_rows:].reshape(
            fracture_low.shape
        ).astype(jnp.bfloat16)
        fracture_padded = jnp.concatenate([fracture_prev, fracture_low, fracture_next_part], 1)
        gathered = jnp.einsum(
            "bkq,fqj->fbkj", rim_onehot, fracture_padded, preferred_element_type=jnp.float32
        ).astype(jnp.bfloat16)
        coupled = jnp.einsum(
            "bkij,fbkj->fbi", fracture_coupling, gathered, preferred_element_type=jnp.float32
        )
        fracture_part = lax.optimization_barrier(source_blocks - coupled)
        leak_fracture = place_values(segment_row_onehot, segment_col_mask, got_rock)
        leak_rock = place_values(
            cell_row_onehot, cell_col_mask, slot_weight_flat[None] * got_fracture
        ).reshape(rock_now.shape)
        fracture_rhs = (fracture_part + leak_fracture).astype(jnp.bfloat16)
        fracture_next = jnp.einsum(
            "bij,fbj->fbi", fracture_inverse, fracture_rhs, preferred_element_type=jnp.float32
        ).reshape(2, -1)
        rock_now, rock_low, rock_high, rock_first, rock_last = rock_step(
            rock_now,
            rock_source,
            leak_rock,
            from_below[:, :layer_rows],
            from_above[:, :layer_rows],
            from_left,
            from_right,
            coef_all,
            cell_inverse,
        )
        fracture_now = fracture_next
    return (rock_now, fracture_now)


def solution(mesh):
    return jax.shard_map(
        shards,
        mesh=mesh,
        in_specs=(
            P(None, "slab", "plane", None),
            P(None, "slab", "plane", None),
            P(None, "slab", "plane", None),
            P(None, "slab", "plane", None),
            P(None, ("slab", "plane")),
            P(None, ("slab", "plane")),
            P(("slab", "plane"), None, None, None),
            P(("slab", "plane"), None, None),
            P(("slab", "plane"), None),
            P("slab", "plane", None),
            P("slab", "plane", None),
            P("slab", "plane", None),
            P("slab", "plane"),
        ),
        out_specs=(P(None, "slab", "plane", None), P(None, ("slab", "plane"))),
        check_vma=False,
    )
```

```python
import jax
import jax.numpy as jnp
from jax import lax
from jax.sharding import PartitionSpec as P

from jax.experimental import pallas as pl
from jax.experimental.pallas import tpu as pltpu


ITERS = 3
INTERPRET = False


def shifted(value, axis, steps):
    count = lax.axis_size(axis)
    first, last = (max(0, -steps), min(count, count - steps))
    return lax.ppermute(value, axis, [(source, source + steps) for source in range(first, last)])


def split_bf16(value):
    high = lax.reduce_precision(value, exponent_bits=8, mantissa_bits=7)
    return high.astype(jnp.bfloat16), (value - high).astype(jnp.bfloat16)


def pick_values(row_onehot, col_mask, table):
    fields = table.shape[0]
    high, low = split_bf16(table)
    parts = jnp.concatenate([high, low], 0)
    by_row = jnp.einsum("kc,grc->grk", col_mask, parts, preferred_element_type=jnp.float32)
    picked = jnp.sum(by_row * row_onehot.astype(jnp.float32)[None], axis=1)
    return picked[:fields] + picked[fields:]


def place_values(row_onehot, col_mask, values):
    fields = values.shape[0]
    high, low = split_bf16(values)
    parts = jnp.concatenate([high, low], 0)
    spread = parts[:, None, :] * row_onehot[None]
    placed = jnp.einsum("grk,kc->grc", spread, col_mask, preferred_element_type=jnp.float32)
    return placed[:fields] + placed[fields:]


def rock_kernel(
    rock_ref, source_ref, leak_ref, below_ref, above_ref, left_ref, right_ref, coef_ref, inv_ref,
    out_ref, low_ref, high_ref, first_ref, last_ref, table_ref,
):
    depth, rows, lanes = rock_ref.shape[1:]
    tiles = leak_ref.shape[2]
    row = lax.broadcasted_iota(jnp.int32, (rows, lanes), 0)
    lane = lax.broadcasted_iota(jnp.int32, (rows, lanes), 1)
    for z in range(depth):
        coef = [coef_ref[d, z].astype(jnp.float32) for d in range(6)]
        rhs = []
        for f in range(2):
            here = rock_ref[f, z]
            down = below_ref[f] if z == 0 else rock_ref[f, z - 1]
            up = above_ref[f] if z == depth - 1 else rock_ref[f, z + 1]
            west = jnp.where(row == 0, left_ref[f, z][None, :], pltpu.roll(here, 1, 0))
            east = jnp.where(row == rows - 1, right_ref[f, z][None, :], pltpu.roll(here, rows - 1, 0))
            south = jnp.where(lane == 0, 0.0, pltpu.roll(here, 1, 1))
            north = jnp.where(lane == lanes - 1, 0.0, pltpu.roll(here, lanes - 1, 1))
            total = coef[0] * down + coef[1] * up + coef[2] * west + coef[3] * east
            total = total + coef[4] * south + coef[5] * north
            leak = jnp.concatenate([leak_ref[f, z, j] for j in range(tiles)], axis=1)
            rhs.append(source_ref[f, z] + total + leak)
        inv = [inv_ref[i, z].astype(jnp.float32) for i in range(4)]
        for f in range(2):
            value = inv[2 * f] * rhs[0] + inv[2 * f + 1] * rhs[1]
            out_ref[f, z] = value
            for j in range(tiles):
                table_ref[f, z, j] = value[:, j * 128 : (j + 1) * 128]
            first_ref[f, z] = value[0]
            last_ref[f, z] = value[rows - 1]
            if z == 0:
                low_ref[f] = value
            if z == depth - 1:
                high_ref[f] = value


def rock_step(rock, source, leak, below, above, left, right, coef, inverse):
    fields, depth, rows, lanes = rock.shape
    vmem = pl.BlockSpec(memory_space=pltpu.VMEM)
    return pl.pallas_call(
        rock_kernel,
        out_shape=(
            jax.ShapeDtypeStruct(rock.shape, jnp.float32),
            jax.ShapeDtypeStruct((fields, rows, lanes), jnp.float32),
            jax.ShapeDtypeStruct((fields, rows, lanes), jnp.float32),
            jax.ShapeDtypeStruct((fields, depth, lanes), jnp.float32),
            jax.ShapeDtypeStruct((fields, depth, lanes), jnp.float32),
            jax.ShapeDtypeStruct(leak.shape, jnp.float32),
        ),
        in_specs=[vmem] * 9,
        out_specs=(vmem,) * 6,
        cost_estimate=pl.CostEstimate(
            flops=40 * rock.size, transcendentals=0, bytes_accessed=20 * rock.size
        ),
        interpret=INTERPRET,
    )(rock, source, leak, below, above, left, right, coef, inverse)


def shards(
    rock_state,
    rock_source,
    transmissibility,
    cell_inverse,
    fracture_state,
    fracture_source,
    fracture_coupling,
    fracture_inverse,
    fracture_neighbours,
    contact_cell,
    contact_segment,
    contact_weight,
    contact_count,
):
    plane_count = lax.axis_size("plane")
    slab_count = lax.axis_size("slab")
    blocks = fracture_coupling.shape[0]
    segment_width = fracture_coupling.shape[-1]
    cell_table = contact_cell[0]
    slot_shape = cell_table.shape
    slot_index = lax.broadcasted_iota(jnp.int32, slot_shape, 1)
    slot_weight = jnp.where(slot_index < contact_count[0][:, None], contact_weight[0], 0.0)
    slot_weight_flat = slot_weight.reshape(-1)
    arrived_segment = lax.all_to_all(
        contact_segment[0], "slab", split_axis=0, concat_axis=0, tiled=True
    )
    my_part = lax.axis_index("slab") * plane_count + lax.axis_index("plane")
    owner_part = fracture_neighbours // blocks
    position = ((owner_part - my_part) // plane_count + 1) * blocks + fracture_neighbours % blocks
    rim_onehot = (
        position[:, :, None] == lax.broadcasted_iota(jnp.int32, (1, 1, 3 * blocks), 2)
    ).astype(jnp.bfloat16)
    cell_total = rock_state[0].size
    cell_rows = cell_total // 128
    cell_flat = cell_table.reshape(-1)
    _, depth, rows, lanes = rock_state.shape
    tiles = lanes // 128
    cell_z = cell_flat // (rows * lanes)
    cell_x = (cell_flat // lanes) % rows
    cell_y = cell_flat % lanes
    cell_row = (cell_z * tiles + cell_y // 128) * rows + cell_x
    cell_row_onehot = (
        cell_row[None, :] == lax.broadcasted_iota(jnp.int32, (cell_rows, 1), 0)
    ).astype(jnp.bfloat16)
    cell_col_mask = (
        (cell_y % 128)[:, None] == lax.broadcasted_iota(jnp.int32, (1, 128), 1)
    ).astype(jnp.bfloat16)
    segment_flat = arrived_segment.reshape(-1)
    segment_row_onehot = (
        (segment_flat // segment_width)[None, :] == lax.broadcasted_iota(jnp.int32, (blocks, 1), 0)
    ).astype(jnp.bfloat16)
    segment_col_mask = (
        (segment_flat % segment_width)[:, None]
        == lax.broadcasted_iota(jnp.int32, (1, segment_width), 1)
    ).astype(jnp.bfloat16)
    coef_z = transmissibility[0]
    coef_x = transmissibility[1]
    coef_y = transmissibility[2]
    layer_above = shifted(transmissibility[0, :1], "slab", -1)
    layer_beside = shifted(transmissibility[1, :, :1], "plane", -1)
    upper_z = jnp.concatenate([coef_z[1:], layer_above], 0)
    upper_x = jnp.concatenate([coef_x[:, 1:], layer_beside], 1)
    upper_y = jnp.pad(coef_y[..., 1:], ((0, 0), (0, 0), (0, 1)))
    forward_slab = [(i, i + 1) for i in range(slab_count - 1)]
    backward_slab = [(i + 1, i) for i in range(slab_count - 1)]
    forward_plane = [(i, i + 1) for i in range(plane_count - 1)]
    backward_plane = [(i + 1, i) for i in range(plane_count - 1)]
    coef_all = jnp.stack([coef_z, upper_z, coef_x, upper_x, coef_y, upper_y])
    rock_now = rock_state
    rock_table = rock_state.reshape(2, depth, rows, tiles, 128).transpose(0, 1, 3, 2, 4)
    rock_table = rock_table.reshape(2, cell_rows, 128)
    rock_low, rock_high = rock_now[:, 0], rock_now[:, -1]
    rock_first, rock_last = rock_now[:, :, 0], rock_now[:, :, -1]
    fracture_now = fracture_state
    source_blocks = fracture_source.reshape(2, blocks, segment_width)
    layer_rows = rock_now.shape[2]
    for _ in range(ITERS):
        rock_picked = pick_values(cell_row_onehot, cell_col_mask, rock_table)
        send_rock = slot_weight_flat[None] * rock_picked
        fracture_table = fracture_now.reshape(2, blocks, segment_width)
        send_fracture = pick_values(segment_row_onehot, segment_col_mask, fracture_table)
        send = jnp.concatenate([send_rock, send_fracture], 0).reshape((4,) + slot_shape)
        got = lax.all_to_all(
            send.transpose(1, 0, 2), "slab", split_axis=0, concat_axis=0, tiled=True
        ).transpose(1, 0, 2)
        got_rock = got[:2].reshape(2, -1)
        got_fracture = got[2:].reshape(2, -1)
        fracture_low = fracture_now.astype(jnp.bfloat16).reshape(2, blocks, segment_width)
        fracture_wide = fracture_low.astype(jnp.float32).reshape(2, -1, rock_now.shape[-1])
        from_below = lax.ppermute(
            jnp.concatenate([rock_high, fracture_wide], 1), "slab", forward_slab
        )
        from_above = lax.ppermute(
            jnp.concatenate([rock_low, fracture_wide], 1), "slab", backward_slab
        )
        from_left = lax.ppermute(rock_last, "plane", forward_plane)
        from_right = lax.ppermute(rock_first, "plane", backward_plane)
        fracture_prev = from_below[:, layer_rows:].reshape(fracture_low.shape).astype(jnp.bfloat16)
        fracture_next_part = from_above[:, layer_rows:].reshape(
            fracture_low.shape
        ).astype(jnp.bfloat16)
        fracture_padded = jnp.concatenate([fracture_prev, fracture_low, fracture_next_part], 1)
        gathered = jnp.einsum(
            "bkq,fqj->fbkj", rim_onehot, fracture_padded, preferred_element_type=jnp.float32
        ).astype(jnp.bfloat16)
        coupled = jnp.einsum(
            "bkij,fbkj->fbi", fracture_coupling, gathered, preferred_element_type=jnp.float32
        )
        fracture_part = lax.optimization_barrier(source_blocks - coupled)
        leak_fracture = place_values(segment_row_onehot, segment_col_mask, got_rock)
        leak_rock = place_values(
            cell_row_onehot, cell_col_mask, slot_weight_flat[None] * got_fracture
        ).reshape(2, depth, tiles, rows, 128)
        fracture_rhs = (fracture_part + leak_fracture).astype(jnp.bfloat16)
        fracture_next = jnp.einsum(
            "bij,fbj->fbi", fracture_inverse, fracture_rhs, preferred_element_type=jnp.float32
        ).reshape(2, -1)
        rock_now, rock_low, rock_high, rock_first, rock_last, rock_table = rock_step(
            rock_now,
            rock_source,
            leak_rock,
            from_below[:, :layer_rows],
            from_above[:, :layer_rows],
            from_left,
            from_right,
            coef_all,
            cell_inverse,
        )
        rock_table = rock_table.reshape(2, cell_rows, 128)
        fracture_now = fracture_next
    return (rock_now, fracture_now)


def solution(mesh):
    return jax.shard_map(
        shards,
        mesh=mesh,
        in_specs=(
            P(None, "slab", "plane", None),
            P(None, "slab", "plane", None),
            P(None, "slab", "plane", None),
            P(None, "slab", "plane", None),
            P(None, ("slab", "plane")),
            P(None, ("slab", "plane")),
            P(("slab", "plane"), None, None, None),
            P(("slab", "plane"), None, None),
            P(("slab", "plane"), None),
            P("slab", "plane", None),
            P("slab", "plane", None),
            P("slab", "plane", None),
            P("slab", "plane"),
        ),
        out_specs=(P(None, "slab", "plane", None), P(None, ("slab", "plane"))),
        check_vma=False,
    )
```

```python
import jax
import jax.numpy as jnp
from jax import lax
from jax.sharding import PartitionSpec as P

from jax.experimental import pallas as pl
from jax.experimental.pallas import tpu as pltpu


ITERS = 3
INTERPRET = False


def shifted(value, axis, steps):
    count = lax.axis_size(axis)
    first, last = (max(0, -steps), min(count, count - steps))
    return lax.ppermute(value, axis, [(source, source + steps) for source in range(first, last)])


def split_bf16(value):
    high = lax.reduce_precision(value, exponent_bits=8, mantissa_bits=7)
    return high.astype(jnp.bfloat16), (value - high).astype(jnp.bfloat16)


def pick_values(row_onehot, col_mask, table):
    fields = table.shape[0]
    high, low = split_bf16(table)
    parts = jnp.concatenate([high, low], 0)
    by_row = jnp.einsum("kc,grc->grk", col_mask, parts, preferred_element_type=jnp.float32)
    picked = jnp.sum(by_row * row_onehot.astype(jnp.float32)[None], axis=1)
    return picked[:fields] + picked[fields:]


def place_values(row_onehot, col_mask, values):
    fields = values.shape[0]
    high, low = split_bf16(values)
    parts = jnp.concatenate([high, low], 0)
    spread = parts[:, None, :] * row_onehot[None]
    placed = jnp.einsum("grk,kc->grc", spread, col_mask, preferred_element_type=jnp.float32)
    return placed[:fields] + placed[fields:]


def rock_kernel(
    rock_ref, source_ref, leak_ref, below_ref, above_ref, left_ref, right_ref, coef_ref, inv_ref,
    out_ref, low_ref, high_ref, first_ref, last_ref, table_ref,
):
    depth, rows, lanes = rock_ref.shape[1:]
    tiles = leak_ref.shape[2]
    row = lax.broadcasted_iota(jnp.int32, (rows, lanes), 0)
    lane = lax.broadcasted_iota(jnp.int32, (rows, lanes), 1)
    for z in range(depth):
        coef = [coef_ref[d, z].astype(jnp.float32) for d in range(6)]
        rhs = []
        for f in range(2):
            here = rock_ref[f, z]
            down = below_ref[f] if z == 0 else rock_ref[f, z - 1]
            up = above_ref[f] if z == depth - 1 else rock_ref[f, z + 1]
            west = jnp.where(row == 0, left_ref[f, z][None, :], pltpu.roll(here, 1, 0))
            east = jnp.where(row == rows - 1, right_ref[f, z][None, :], pltpu.roll(here, rows - 1, 0))
            south = jnp.where(lane == 0, 0.0, pltpu.roll(here, 1, 1))
            north = jnp.where(lane == lanes - 1, 0.0, pltpu.roll(here, lanes - 1, 1))
            total = coef[0] * down + coef[1] * up + coef[2] * west + coef[3] * east
            total = total + coef[4] * south + coef[5] * north
            leak = jnp.concatenate([leak_ref[f, z, j] for j in range(tiles)], axis=1)
            rhs.append(source_ref[f, z] + total + leak)
        inv = [inv_ref[i, z].astype(jnp.float32) for i in range(4)]
        for f in range(2):
            value = inv[2 * f] * rhs[0] + inv[2 * f + 1] * rhs[1]
            out_ref[f, z] = value
            for j in range(tiles):
                table_ref[f, z, j] = value[:, j * 128 : (j + 1) * 128]
            first_ref[f, z] = value[0]
            last_ref[f, z] = value[rows - 1]
            if z == 0:
                low_ref[f] = value
            if z == depth - 1:
                high_ref[f] = value


def rock_step(rock, source, leak, below, above, left, right, coef, inverse):
    fields, depth, rows, lanes = rock.shape
    vmem = pl.BlockSpec(memory_space=pltpu.VMEM)
    return pl.pallas_call(
        rock_kernel,
        out_shape=(
            jax.ShapeDtypeStruct(rock.shape, jnp.float32),
            jax.ShapeDtypeStruct((fields, rows, lanes), jnp.float32),
            jax.ShapeDtypeStruct((fields, rows, lanes), jnp.float32),
            jax.ShapeDtypeStruct((fields, depth, lanes), jnp.float32),
            jax.ShapeDtypeStruct((fields, depth, lanes), jnp.float32),
            jax.ShapeDtypeStruct(leak.shape, jnp.float32),
        ),
        in_specs=[vmem] * 9,
        out_specs=(vmem,) * 6,
        cost_estimate=pl.CostEstimate(
            flops=40 * rock.size, transcendentals=0, bytes_accessed=20 * rock.size
        ),
        interpret=INTERPRET,
    )(rock, source, leak, below, above, left, right, coef, inverse)


def shards(
    rock_state,
    rock_source,
    transmissibility,
    cell_inverse,
    fracture_state,
    fracture_source,
    fracture_coupling,
    fracture_inverse,
    fracture_neighbours,
    contact_cell,
    contact_segment,
    contact_weight,
    contact_count,
):
    plane_count = lax.axis_size("plane")
    slab_count = lax.axis_size("slab")
    blocks = fracture_coupling.shape[0]
    segment_width = fracture_coupling.shape[-1]
    cell_table = contact_cell[0]
    slot_shape = cell_table.shape
    slot_index = lax.broadcasted_iota(jnp.int32, slot_shape, 1)
    slot_weight = jnp.where(slot_index < contact_count[0][:, None], contact_weight[0], 0.0)
    slot_weight_flat = slot_weight.reshape(-1)
    arrived_segment = lax.all_to_all(
        contact_segment[0], "slab", split_axis=0, concat_axis=0, tiled=True
    )
    my_part = lax.axis_index("slab") * plane_count + lax.axis_index("plane")
    owner_part = fracture_neighbours // blocks
    position = ((owner_part - my_part) // plane_count + 1) * blocks + fracture_neighbours % blocks
    rim_onehot = (
        position[:, :, None] == lax.broadcasted_iota(jnp.int32, (1, 1, 3 * blocks), 2)
    ).astype(jnp.bfloat16)
    cell_total = rock_state[0].size
    cell_rows = cell_total // 128
    cell_flat = cell_table.reshape(-1)
    _, depth, rows, lanes = rock_state.shape
    tiles = lanes // 128
    cell_z = cell_flat // (rows * lanes)
    cell_x = (cell_flat // lanes) % rows
    cell_y = cell_flat % lanes
    cell_row = (cell_z * tiles + cell_y // 128) * rows + cell_x
    cell_row_onehot = (
        cell_row[None, :] == lax.broadcasted_iota(jnp.int32, (cell_rows, 1), 0)
    ).astype(jnp.bfloat16)
    cell_col_mask = (
        (cell_y % 128)[:, None] == lax.broadcasted_iota(jnp.int32, (1, 128), 1)
    ).astype(jnp.bfloat16)
    segment_flat = arrived_segment.reshape(-1)
    segment_row_onehot = (
        (segment_flat // segment_width)[None, :] == lax.broadcasted_iota(jnp.int32, (blocks, 1), 0)
    ).astype(jnp.bfloat16)
    segment_col_mask = (
        (segment_flat % segment_width)[:, None]
        == lax.broadcasted_iota(jnp.int32, (1, segment_width), 1)
    ).astype(jnp.bfloat16)
    coef_z = transmissibility[0]
    coef_x = transmissibility[1]
    coef_y = transmissibility[2]
    forward_slab = [(i, i + 1) for i in range(slab_count - 1)]
    backward_slab = [(i + 1, i) for i in range(slab_count - 1)]
    forward_plane = [(i, i + 1) for i in range(plane_count - 1)]
    backward_plane = [(i + 1, i) for i in range(plane_count - 1)]
    rock_now = rock_state
    rock_table = rock_state.reshape(2, depth, rows, tiles, 128).transpose(0, 1, 3, 2, 4)
    rock_table = rock_table.reshape(2, cell_rows, 128)
    rock_low, rock_high = rock_now[:, 0], rock_now[:, -1]
    rock_first, rock_last = rock_now[:, :, 0], rock_now[:, :, -1]
    fracture_now = fracture_state
    source_blocks = fracture_source.reshape(2, blocks, segment_width)
    layer_rows = rock_now.shape[2]
    for sweep_index in range(ITERS):
        rock_picked = pick_values(cell_row_onehot, cell_col_mask, rock_table)
        send_rock = slot_weight_flat[None] * rock_picked
        fracture_table = fracture_now.reshape(2, blocks, segment_width)
        send_fracture = pick_values(segment_row_onehot, segment_col_mask, fracture_table)
        send = jnp.concatenate([send_rock, send_fracture], 0).reshape((4,) + slot_shape)
        got = lax.all_to_all(
            send.transpose(1, 0, 2), "slab", split_axis=0, concat_axis=0, tiled=True
        ).transpose(1, 0, 2)
        got_rock = got[:2].reshape(2, -1)
        got_fracture = got[2:].reshape(2, -1)
        fracture_low = fracture_now.astype(jnp.bfloat16).reshape(2, blocks, segment_width)
        fracture_wide = fracture_low.astype(jnp.float32).reshape(2, -1, rock_now.shape[-1])
        from_left = lax.ppermute(rock_last, "plane", forward_plane)
        from_right = lax.ppermute(rock_first, "plane", backward_plane)
        if sweep_index == 0:
            layer_beside = shifted(transmissibility[1, :, :1], "plane", -1)
        from_below = lax.ppermute(
            jnp.concatenate([rock_high, fracture_wide], 1), "slab", forward_slab
        )
        from_above = lax.ppermute(
            jnp.concatenate([rock_low, fracture_wide], 1), "slab", backward_slab
        )
        if sweep_index == 0:
            layer_above = shifted(transmissibility[0, :1], "slab", -1)
        if sweep_index == 0:
            upper_z = jnp.concatenate([coef_z[1:], layer_above], 0)
            upper_x = jnp.concatenate([coef_x[:, 1:], layer_beside], 1)
            upper_y = jnp.pad(coef_y[..., 1:], ((0, 0), (0, 0), (0, 1)))
            coef_all = jnp.stack([coef_z, upper_z, coef_x, upper_x, coef_y, upper_y])
        fracture_prev = from_below[:, layer_rows:].reshape(fracture_low.shape).astype(jnp.bfloat16)
        fracture_next_part = from_above[:, layer_rows:].reshape(
            fracture_low.shape
        ).astype(jnp.bfloat16)
        fracture_padded = jnp.concatenate([fracture_prev, fracture_low, fracture_next_part], 1)
        gathered = jnp.einsum(
            "bkq,fqj->fbkj", rim_onehot, fracture_padded, preferred_element_type=jnp.float32
        ).astype(jnp.bfloat16)
        coupled = jnp.einsum(
            "bkij,fbkj->fbi", fracture_coupling, gathered, preferred_element_type=jnp.float32
        )
        fracture_part = lax.optimization_barrier(source_blocks - coupled)
        leak_fracture = place_values(segment_row_onehot, segment_col_mask, got_rock)
        leak_rock = place_values(
            cell_row_onehot, cell_col_mask, slot_weight_flat[None] * got_fracture
        ).reshape(2, depth, tiles, rows, 128)
        fracture_rhs = (fracture_part + leak_fracture).astype(jnp.bfloat16)
        fracture_next = jnp.einsum(
            "bij,fbj->fbi", fracture_inverse, fracture_rhs, preferred_element_type=jnp.float32
        ).reshape(2, -1)
        rock_now, rock_low, rock_high, rock_first, rock_last, rock_table = rock_step(
            rock_now,
            rock_source,
            leak_rock,
            from_below[:, :layer_rows],
            from_above[:, :layer_rows],
            from_left,
            from_right,
            coef_all,
            cell_inverse,
        )
        rock_table = rock_table.reshape(2, cell_rows, 128)
        fracture_now = fracture_next
    return (rock_now, fracture_now)


def solution(mesh):
    return jax.shard_map(
        shards,
        mesh=mesh,
        in_specs=(
            P(None, "slab", "plane", None),
            P(None, "slab", "plane", None),
            P(None, "slab", "plane", None),
            P(None, "slab", "plane", None),
            P(None, ("slab", "plane")),
            P(None, ("slab", "plane")),
            P(("slab", "plane"), None, None, None),
            P(("slab", "plane"), None, None),
            P(("slab", "plane"), None),
            P("slab", "plane", None),
            P("slab", "plane", None),
            P("slab", "plane", None),
            P("slab", "plane"),
        ),
        out_specs=(P(None, "slab", "plane", None), P(None, ("slab", "plane"))),
        check_vma=False,
    )
```

```python
import jax
import jax.numpy as jnp
from jax import lax
from jax.sharding import PartitionSpec as P

from jax.experimental import pallas as pl
from jax.experimental.pallas import tpu as pltpu


ITERS = 3
INTERPRET = False


def shifted(value, axis, steps):
    count = lax.axis_size(axis)
    first, last = (max(0, -steps), min(count, count - steps))
    return lax.ppermute(value, axis, [(source, source + steps) for source in range(first, last)])


def split_bf16(value):
    high = lax.reduce_precision(value, exponent_bits=8, mantissa_bits=7)
    return high.astype(jnp.bfloat16), (value - high).astype(jnp.bfloat16)


def pick_values(row_onehot, col_mask, table):
    fields = table.shape[0]
    high, low = split_bf16(table)
    parts = jnp.concatenate([high, low], 0)
    by_row = jnp.einsum("kc,grc->grk", col_mask, parts, preferred_element_type=jnp.float32)
    picked = jnp.sum(by_row * row_onehot.astype(jnp.float32)[None], axis=1)
    return picked[:fields] + picked[fields:]


def place_values(row_onehot, col_mask, values):
    fields = values.shape[0]
    high, low = split_bf16(values)
    parts = jnp.concatenate([high, low], 0)
    spread = parts[:, None, :] * row_onehot[None]
    placed = jnp.einsum("grk,kc->grc", spread, col_mask, preferred_element_type=jnp.float32)
    return placed[:fields] + placed[fields:]


def rock_kernel(
    rock_ref, source_ref, leak_ref, below_ref, above_ref, left_ref, right_ref, coef_ref, inv_ref,
    out_ref, low_ref, high_ref, first_ref, last_ref, table_ref,
):
    depth, rows, lanes = rock_ref.shape[1:]
    tiles = leak_ref.shape[2]
    row = lax.broadcasted_iota(jnp.int32, (rows, lanes), 0)
    lane = lax.broadcasted_iota(jnp.int32, (rows, lanes), 1)
    for z in range(depth):
        coef = [coef_ref[d, z].astype(jnp.float32) for d in range(6)]
        rhs = []
        for f in range(2):
            here = rock_ref[f, z]
            down = below_ref[f, :rows] if z == 0 else rock_ref[f, z - 1]
            up = above_ref[f, :rows] if z == depth - 1 else rock_ref[f, z + 1]
            west = jnp.where(row == 0, left_ref[f, z][None, :], pltpu.roll(here, 1, 0))
            east = jnp.where(row == rows - 1, right_ref[f, z][None, :], pltpu.roll(here, rows - 1, 0))
            south = jnp.where(lane == 0, 0.0, pltpu.roll(here, 1, 1))
            north = jnp.where(lane == lanes - 1, 0.0, pltpu.roll(here, lanes - 1, 1))
            total = coef[0] * down + coef[1] * up + coef[2] * west + coef[3] * east
            total = total + coef[4] * south + coef[5] * north
            leak = jnp.concatenate([leak_ref[f, z, j] for j in range(tiles)], axis=1)
            rhs.append(source_ref[f, z] + total + leak)
        inv = [inv_ref[i, z].astype(jnp.float32) for i in range(4)]
        for f in range(2):
            value = inv[2 * f] * rhs[0] + inv[2 * f + 1] * rhs[1]
            out_ref[f, z] = value
            for j in range(tiles):
                table_ref[f, z, j] = value[:, j * 128 : (j + 1) * 128]
            first_ref[f, z] = value[0]
            last_ref[f, z] = value[rows - 1]
            if z == 0:
                low_ref[f] = value
            if z == depth - 1:
                high_ref[f] = value


def rock_step(rock, source, leak, below, above, left, right, coef, inverse):
    fields, depth, rows, lanes = rock.shape
    vmem = pl.BlockSpec(memory_space=pltpu.VMEM)
    return pl.pallas_call(
        rock_kernel,
        out_shape=(
            jax.ShapeDtypeStruct(rock.shape, jnp.float32),
            jax.ShapeDtypeStruct((fields, rows, lanes), jnp.float32),
            jax.ShapeDtypeStruct((fields, rows, lanes), jnp.float32),
            jax.ShapeDtypeStruct((fields, depth, lanes), jnp.float32),
            jax.ShapeDtypeStruct((fields, depth, lanes), jnp.float32),
            jax.ShapeDtypeStruct(leak.shape, jnp.float32),
        ),
        in_specs=[vmem] * 9,
        out_specs=(vmem,) * 6,
        cost_estimate=pl.CostEstimate(
            flops=40 * rock.size, transcendentals=0, bytes_accessed=20 * rock.size
        ),
        interpret=INTERPRET,
    )(rock, source, leak, below, above, left, right, coef, inverse)


def shards(
    rock_state,
    rock_source,
    transmissibility,
    cell_inverse,
    fracture_state,
    fracture_source,
    fracture_coupling,
    fracture_inverse,
    fracture_neighbours,
    contact_cell,
    contact_segment,
    contact_weight,
    contact_count,
):
    plane_count = lax.axis_size("plane")
    slab_count = lax.axis_size("slab")
    blocks = fracture_coupling.shape[0]
    segment_width = fracture_coupling.shape[-1]
    cell_table = contact_cell[0]
    slot_shape = cell_table.shape
    slot_index = lax.broadcasted_iota(jnp.int32, slot_shape, 1)
    slot_weight = jnp.where(slot_index < contact_count[0][:, None], contact_weight[0], 0.0)
    slot_weight_flat = slot_weight.reshape(-1)
    arrived_segment = lax.all_to_all(
        contact_segment[0], "slab", split_axis=0, concat_axis=0, tiled=True
    )
    my_part = lax.axis_index("slab") * plane_count + lax.axis_index("plane")
    owner_part = fracture_neighbours // blocks
    position = ((owner_part - my_part) // plane_count + 1) * blocks + fracture_neighbours % blocks
    rim_onehot = (
        position[:, :, None] == lax.broadcasted_iota(jnp.int32, (1, 1, 3 * blocks), 2)
    ).astype(jnp.bfloat16)
    cell_total = rock_state[0].size
    cell_rows = cell_total // 128
    cell_flat = cell_table.reshape(-1)
    _, depth, rows, lanes = rock_state.shape
    tiles = lanes // 128
    cell_z = cell_flat // (rows * lanes)
    cell_x = (cell_flat // lanes) % rows
    cell_y = cell_flat % lanes
    cell_row = (cell_z * tiles + cell_y // 128) * rows + cell_x
    cell_row_onehot = (
        cell_row[None, :] == lax.broadcasted_iota(jnp.int32, (cell_rows, 1), 0)
    ).astype(jnp.bfloat16)
    cell_col_mask = (
        (cell_y % 128)[:, None] == lax.broadcasted_iota(jnp.int32, (1, 128), 1)
    ).astype(jnp.bfloat16)
    segment_flat = arrived_segment.reshape(-1)
    segment_row_onehot = (
        (segment_flat // segment_width)[None, :] == lax.broadcasted_iota(jnp.int32, (blocks, 1), 0)
    ).astype(jnp.bfloat16)
    segment_col_mask = (
        (segment_flat % segment_width)[:, None]
        == lax.broadcasted_iota(jnp.int32, (1, segment_width), 1)
    ).astype(jnp.bfloat16)
    coef_z = transmissibility[0]
    coef_x = transmissibility[1]
    coef_y = transmissibility[2]
    forward_slab = [(i, i + 1) for i in range(slab_count - 1)]
    backward_slab = [(i + 1, i) for i in range(slab_count - 1)]
    forward_plane = [(i, i + 1) for i in range(plane_count - 1)]
    backward_plane = [(i + 1, i) for i in range(plane_count - 1)]
    rock_now = rock_state
    rock_table = rock_state.reshape(2, depth, rows, tiles, 128).transpose(0, 1, 3, 2, 4)
    rock_table = rock_table.reshape(2, cell_rows, 128)
    rock_low, rock_high = rock_now[:, 0], rock_now[:, -1]
    rock_first, rock_last = rock_now[:, :, 0], rock_now[:, :, -1]
    fracture_now = fracture_state
    source_blocks = fracture_source.reshape(2, blocks, segment_width)
    layer_rows = rock_now.shape[2]
    for sweep_index in range(ITERS):
        rock_picked = pick_values(cell_row_onehot, cell_col_mask, rock_table)
        send_rock = slot_weight_flat[None] * rock_picked
        fracture_table = fracture_now.reshape(2, blocks, segment_width)
        send_fracture = pick_values(segment_row_onehot, segment_col_mask, fracture_table)
        send = jnp.concatenate([send_rock, send_fracture], 0).reshape((4,) + slot_shape)
        got = lax.all_to_all(
            send.transpose(1, 0, 2), "slab", split_axis=0, concat_axis=0, tiled=True
        ).transpose(1, 0, 2)
        got_rock = got[:2].reshape(2, -1)
        got_fracture = got[2:].reshape(2, -1)
        fracture_low = fracture_now.astype(jnp.bfloat16).reshape(2, blocks, segment_width)
        fracture_wide = fracture_low.astype(jnp.float32).reshape(2, -1, rock_now.shape[-1])
        from_below = lax.ppermute(
            jnp.concatenate([rock_high, fracture_wide], 1), "slab", forward_slab
        )
        from_above = lax.ppermute(
            jnp.concatenate([rock_low, fracture_wide], 1), "slab", backward_slab
        )
        from_left = lax.ppermute(rock_last, "plane", forward_plane)
        from_right = lax.ppermute(rock_first, "plane", backward_plane)
        if sweep_index == 0:
            layer_above = shifted(transmissibility[0, :1], "slab", -1)
            layer_beside = shifted(transmissibility[1, :, :1], "plane", -1)
            upper_z = jnp.concatenate([coef_z[1:], layer_above], 0)
            upper_x = jnp.concatenate([coef_x[:, 1:], layer_beside], 1)
            upper_y = jnp.pad(coef_y[..., 1:], ((0, 0), (0, 0), (0, 1)))
            coef_all = jnp.stack([coef_z, upper_z, coef_x, upper_x, coef_y, upper_y])
        fracture_prev = from_below[:, layer_rows:].reshape(fracture_low.shape).astype(jnp.bfloat16)
        fracture_next_part = from_above[:, layer_rows:].reshape(
            fracture_low.shape
        ).astype(jnp.bfloat16)
        fracture_padded = jnp.concatenate([fracture_prev, fracture_low, fracture_next_part], 1)
        gathered = jnp.einsum(
            "bkq,fqj->fbkj", rim_onehot, fracture_padded, preferred_element_type=jnp.float32
        ).astype(jnp.bfloat16)
        coupled = jnp.einsum(
            "bkij,fbkj->fbi", fracture_coupling, gathered, preferred_element_type=jnp.float32
        )
        fracture_part = lax.optimization_barrier(source_blocks - coupled)
        leak_fracture = place_values(segment_row_onehot, segment_col_mask, got_rock)
        leak_rock = place_values(
            cell_row_onehot, cell_col_mask, slot_weight_flat[None] * got_fracture
        ).reshape(2, depth, tiles, rows, 128)
        fracture_rhs = (fracture_part + leak_fracture).astype(jnp.bfloat16)
        fracture_next = jnp.einsum(
            "bij,fbj->fbi", fracture_inverse, fracture_rhs, preferred_element_type=jnp.float32
        ).reshape(2, -1)
        rock_now, rock_low, rock_high, rock_first, rock_last, rock_table = rock_step(
            rock_now,
            rock_source,
            leak_rock,
            from_below,
            from_above,
            from_left,
            from_right,
            coef_all,
            cell_inverse,
        )
        rock_table = rock_table.reshape(2, cell_rows, 128)
        fracture_now = fracture_next
    return (rock_now, fracture_now)


def solution(mesh):
    return jax.shard_map(
        shards,
        mesh=mesh,
        in_specs=(
            P(None, "slab", "plane", None),
            P(None, "slab", "plane", None),
            P(None, "slab", "plane", None),
            P(None, "slab", "plane", None),
            P(None, ("slab", "plane")),
            P(None, ("slab", "plane")),
            P(("slab", "plane"), None, None, None),
            P(("slab", "plane"), None, None),
            P(("slab", "plane"), None),
            P("slab", "plane", None),
            P("slab", "plane", None),
            P("slab", "plane", None),
            P("slab", "plane"),
        ),
        out_specs=(P(None, "slab", "plane", None), P(None, ("slab", "plane"))),
        check_vma=False,
    )
```

```python
import jax
import jax.numpy as jnp
from jax import lax
from jax.sharding import PartitionSpec as P

from jax.experimental import pallas as pl
from jax.experimental.pallas import tpu as pltpu


ITERS = 3
INTERPRET = False


def shifted(value, axis, steps):
    count = lax.axis_size(axis)
    first, last = (max(0, -steps), min(count, count - steps))
    return lax.ppermute(value, axis, [(source, source + steps) for source in range(first, last)])


def split_bf16(value):
    high = lax.reduce_precision(value, exponent_bits=8, mantissa_bits=7)
    return high.astype(jnp.bfloat16), (value - high).astype(jnp.bfloat16)


def pick_values(row_onehot, col_mask, table):
    fields = table.shape[0]
    high, low = split_bf16(table)
    parts = jnp.concatenate([high, low], 0)
    by_row = jnp.einsum("kc,grc->grk", col_mask, parts, preferred_element_type=jnp.float32)
    picked = jnp.sum(by_row * row_onehot.astype(jnp.float32)[None], axis=1)
    return picked[:fields] + picked[fields:]


def place_values(row_onehot, col_mask, values):
    fields = values.shape[0]
    high, low = split_bf16(values)
    parts = jnp.concatenate([high, low], 0)
    spread = parts[:, None, :] * row_onehot[None]
    placed = jnp.einsum("grk,kc->grc", spread, col_mask, preferred_element_type=jnp.float32)
    return placed[:fields] + placed[fields:]


def rock_kernel(
    rock_ref, source_ref, leak_ref, below_ref, above_ref, left_ref, right_ref, coef_ref, inv_ref,
    fracture_ref, out_ref, low_ref, high_ref, first_ref, last_ref, table_ref,
):
    depth, rows, lanes = rock_ref.shape[1:]
    tiles = leak_ref.shape[2]
    row = lax.broadcasted_iota(jnp.int32, (rows, lanes), 0)
    lane = lax.broadcasted_iota(jnp.int32, (rows, lanes), 1)
    for z in range(depth):
        coef = [coef_ref[d, z].astype(jnp.float32) for d in range(6)]
        rhs = []
        for f in range(2):
            here = rock_ref[f, z]
            down = below_ref[f, :rows] if z == 0 else rock_ref[f, z - 1]
            up = above_ref[f, :rows] if z == depth - 1 else rock_ref[f, z + 1]
            west = jnp.where(row == 0, left_ref[f, z][None, :], pltpu.roll(here, 1, 0))
            east = jnp.where(row == rows - 1, right_ref[f, z][None, :], pltpu.roll(here, rows - 1, 0))
            south = jnp.where(lane == 0, 0.0, pltpu.roll(here, 1, 1))
            north = jnp.where(lane == lanes - 1, 0.0, pltpu.roll(here, lanes - 1, 1))
            total = coef[0] * down + coef[1] * up + coef[2] * west + coef[3] * east
            total = total + coef[4] * south + coef[5] * north
            leak = jnp.concatenate([leak_ref[f, z, j] for j in range(tiles)], axis=1)
            rhs.append(source_ref[f, z] + total + leak)
        inv = [inv_ref[i, z].astype(jnp.float32) for i in range(4)]
        for f in range(2):
            value = inv[2 * f] * rhs[0] + inv[2 * f + 1] * rhs[1]
            out_ref[f, z] = value
            for j in range(tiles):
                table_ref[f, z, j] = value[:, j * 128 : (j + 1) * 128]
            first_ref[f, z] = value[0]
            last_ref[f, z] = value[rows - 1]
            if z == 0:
                low_ref[f, :rows] = value
                low_ref[f, rows:] = fracture_ref[f]
            if z == depth - 1:
                high_ref[f, :rows] = value
                high_ref[f, rows:] = fracture_ref[f]


def rock_step(rock, source, leak, below, above, left, right, coef, inverse, fracture):
    fields, depth, rows, lanes = rock.shape
    halo_rows = rows + fracture.shape[1]
    vmem = pl.BlockSpec(memory_space=pltpu.VMEM)
    return pl.pallas_call(
        rock_kernel,
        out_shape=(
            jax.ShapeDtypeStruct(rock.shape, jnp.float32),
            jax.ShapeDtypeStruct((fields, halo_rows, lanes), jnp.float32),
            jax.ShapeDtypeStruct((fields, halo_rows, lanes), jnp.float32),
            jax.ShapeDtypeStruct((fields, depth, lanes), jnp.float32),
            jax.ShapeDtypeStruct((fields, depth, lanes), jnp.float32),
            jax.ShapeDtypeStruct(leak.shape, jnp.float32),
        ),
        in_specs=[vmem] * 10,
        out_specs=(vmem,) * 6,
        cost_estimate=pl.CostEstimate(
            flops=40 * rock.size, transcendentals=0, bytes_accessed=20 * rock.size
        ),
        interpret=INTERPRET,
    )(rock, source, leak, below, above, left, right, coef, inverse, fracture)


def shards(
    rock_state,
    rock_source,
    transmissibility,
    cell_inverse,
    fracture_state,
    fracture_source,
    fracture_coupling,
    fracture_inverse,
    fracture_neighbours,
    contact_cell,
    contact_segment,
    contact_weight,
    contact_count,
):
    plane_count = lax.axis_size("plane")
    slab_count = lax.axis_size("slab")
    blocks = fracture_coupling.shape[0]
    segment_width = fracture_coupling.shape[-1]
    cell_table = contact_cell[0]
    slot_shape = cell_table.shape
    slot_index = lax.broadcasted_iota(jnp.int32, slot_shape, 1)
    slot_weight = jnp.where(slot_index < contact_count[0][:, None], contact_weight[0], 0.0)
    slot_weight_flat = slot_weight.reshape(-1)
    arrived_segment = lax.all_to_all(
        contact_segment[0], "slab", split_axis=0, concat_axis=0, tiled=True
    )
    my_part = lax.axis_index("slab") * plane_count + lax.axis_index("plane")
    owner_part = fracture_neighbours // blocks
    position = ((owner_part - my_part) // plane_count + 1) * blocks + fracture_neighbours % blocks
    rim_onehot = (
        position[:, :, None] == lax.broadcasted_iota(jnp.int32, (1, 1, 3 * blocks), 2)
    ).astype(jnp.bfloat16)
    cell_total = rock_state[0].size
    cell_rows = cell_total // 128
    cell_flat = cell_table.reshape(-1)
    _, depth, rows, lanes = rock_state.shape
    tiles = lanes // 128
    cell_z = cell_flat // (rows * lanes)
    cell_x = (cell_flat // lanes) % rows
    cell_y = cell_flat % lanes
    cell_row = (cell_z * tiles + cell_y // 128) * rows + cell_x
    cell_row_onehot = (
        cell_row[None, :] == lax.broadcasted_iota(jnp.int32, (cell_rows, 1), 0)
    ).astype(jnp.bfloat16)
    cell_col_mask = (
        (cell_y % 128)[:, None] == lax.broadcasted_iota(jnp.int32, (1, 128), 1)
    ).astype(jnp.bfloat16)
    segment_flat = arrived_segment.reshape(-1)
    segment_row_onehot = (
        (segment_flat // segment_width)[None, :] == lax.broadcasted_iota(jnp.int32, (blocks, 1), 0)
    ).astype(jnp.bfloat16)
    segment_col_mask = (
        (segment_flat % segment_width)[:, None]
        == lax.broadcasted_iota(jnp.int32, (1, segment_width), 1)
    ).astype(jnp.bfloat16)
    coef_z = transmissibility[0]
    coef_x = transmissibility[1]
    coef_y = transmissibility[2]
    forward_slab = [(i, i + 1) for i in range(slab_count - 1)]
    backward_slab = [(i + 1, i) for i in range(slab_count - 1)]
    forward_plane = [(i, i + 1) for i in range(plane_count - 1)]
    backward_plane = [(i + 1, i) for i in range(plane_count - 1)]
    rock_now = rock_state
    rock_table = rock_state.reshape(2, depth, rows, tiles, 128).transpose(0, 1, 3, 2, 4)
    rock_table = rock_table.reshape(2, cell_rows, 128)
    fracture_start = fracture_state.astype(jnp.bfloat16).astype(jnp.float32)
    fracture_start = fracture_start.reshape(2, -1, rock_state.shape[-1])
    rock_low = jnp.concatenate([rock_now[:, 0], fracture_start], 1)
    rock_high = jnp.concatenate([rock_now[:, -1], fracture_start], 1)
    rock_first, rock_last = rock_now[:, :, 0], rock_now[:, :, -1]
    fracture_now = fracture_state
    source_blocks = fracture_source.reshape(2, blocks, segment_width)
    layer_rows = rock_now.shape[2]
    for sweep_index in range(ITERS):
        rock_picked = pick_values(cell_row_onehot, cell_col_mask, rock_table)
        send_rock = slot_weight_flat[None] * rock_picked
        fracture_table = fracture_now.reshape(2, blocks, segment_width)
        send_fracture = pick_values(segment_row_onehot, segment_col_mask, fracture_table)
        send = jnp.concatenate([send_rock, send_fracture], 0).reshape((4,) + slot_shape)
        got = lax.all_to_all(
            send.transpose(1, 0, 2), "slab", split_axis=0, concat_axis=0, tiled=True
        ).transpose(1, 0, 2)
        got_rock = got[:2].reshape(2, -1)
        got_fracture = got[2:].reshape(2, -1)
        fracture_low = fracture_now.astype(jnp.bfloat16).reshape(2, blocks, segment_width)
        fracture_wide = fracture_low.astype(jnp.float32).reshape(2, -1, rock_now.shape[-1])
        from_below = lax.ppermute(rock_high, "slab", forward_slab)
        from_above = lax.ppermute(rock_low, "slab", backward_slab)
        from_left = lax.ppermute(rock_last, "plane", forward_plane)
        from_right = lax.ppermute(rock_first, "plane", backward_plane)
        if sweep_index == 0:
            layer_above = shifted(transmissibility[0, :1], "slab", -1)
            layer_beside = shifted(transmissibility[1, :, :1], "plane", -1)
            upper_z = jnp.concatenate([coef_z[1:], layer_above], 0)
            upper_x = jnp.concatenate([coef_x[:, 1:], layer_beside], 1)
            upper_y = jnp.pad(coef_y[..., 1:], ((0, 0), (0, 0), (0, 1)))
            coef_all = jnp.stack([coef_z, upper_z, coef_x, upper_x, coef_y, upper_y])
        fracture_prev = from_below[:, layer_rows:].reshape(fracture_low.shape).astype(jnp.bfloat16)
        fracture_next_part = from_above[:, layer_rows:].reshape(
            fracture_low.shape
        ).astype(jnp.bfloat16)
        fracture_padded = jnp.concatenate([fracture_prev, fracture_low, fracture_next_part], 1)
        gathered = jnp.einsum(
            "bkq,fqj->fbkj", rim_onehot, fracture_padded, preferred_element_type=jnp.float32
        ).astype(jnp.bfloat16)
        coupled = jnp.einsum(
            "bkij,fbkj->fbi", fracture_coupling, gathered, preferred_element_type=jnp.float32
        )
        fracture_part = lax.optimization_barrier(source_blocks - coupled)
        leak_fracture = place_values(segment_row_onehot, segment_col_mask, got_rock)
        leak_rock = place_values(
            cell_row_onehot, cell_col_mask, slot_weight_flat[None] * got_fracture
        ).reshape(2, depth, tiles, rows, 128)
        fracture_rhs = (fracture_part + leak_fracture).astype(jnp.bfloat16)
        fracture_next = jnp.einsum(
            "bij,fbj->fbi", fracture_inverse, fracture_rhs, preferred_element_type=jnp.float32
        ).reshape(2, -1)
        rock_now, rock_low, rock_high, rock_first, rock_last, rock_table = rock_step(
            rock_now,
            rock_source,
            leak_rock,
            from_below,
            from_above,
            from_left,
            from_right,
            coef_all,
            cell_inverse,
            fracture_next.astype(jnp.bfloat16).astype(jnp.float32).reshape(fracture_wide.shape),
        )
        rock_table = rock_table.reshape(2, cell_rows, 128)
        fracture_now = fracture_next
    return (rock_now, fracture_now)


def solution(mesh):
    return jax.shard_map(
        shards,
        mesh=mesh,
        in_specs=(
            P(None, "slab", "plane", None),
            P(None, "slab", "plane", None),
            P(None, "slab", "plane", None),
            P(None, "slab", "plane", None),
            P(None, ("slab", "plane")),
            P(None, ("slab", "plane")),
            P(("slab", "plane"), None, None, None),
            P(("slab", "plane"), None, None),
            P(("slab", "plane"), None),
            P("slab", "plane", None),
            P("slab", "plane", None),
            P("slab", "plane", None),
            P("slab", "plane"),
        ),
        out_specs=(P(None, "slab", "plane", None), P(None, ("slab", "plane"))),
        check_vma=False,
    )
```

```python
import jax
import jax.numpy as jnp
from jax import lax
from jax.sharding import PartitionSpec as P

from jax.experimental import pallas as pl
from jax.experimental.pallas import tpu as pltpu


ITERS = 3
INTERPRET = False


def shifted(value, axis, steps):
    count = lax.axis_size(axis)
    first, last = (max(0, -steps), min(count, count - steps))
    return lax.ppermute(value, axis, [(source, source + steps) for source in range(first, last)])


def split_bf16(value):
    high = lax.reduce_precision(value, exponent_bits=8, mantissa_bits=7)
    return high.astype(jnp.bfloat16), (value - high).astype(jnp.bfloat16)


def pick_values(row_onehot, col_mask, table):
    high, low = split_bf16(table)
    return pick_parts(row_onehot, col_mask, jnp.concatenate([high, low], 0))


def pick_parts(row_onehot, col_mask, parts):
    fields = parts.shape[0] // 2
    by_row = jnp.einsum("kc,grc->grk", col_mask, parts, preferred_element_type=jnp.float32)
    picked = jnp.sum(by_row * row_onehot.astype(jnp.float32)[None], axis=1)
    return picked[:fields] + picked[fields:]


def place_values(row_onehot, col_mask, values):
    fields = values.shape[0]
    high, low = split_bf16(values)
    parts = jnp.concatenate([high, low], 0)
    spread = parts[:, None, :] * row_onehot[None]
    placed = jnp.einsum("grk,kc->grc", spread, col_mask, preferred_element_type=jnp.float32)
    return placed[:fields] + placed[fields:]


def rock_kernel(
    rock_ref, source_ref, leak_ref, below_ref, above_ref, left_ref, right_ref, coef_ref, inv_ref,
    fracture_ref, out_ref, low_ref, high_ref, first_ref, last_ref, table_ref,
):
    fields, depth, rows, lanes = rock_ref.shape
    tiles = leak_ref.shape[2]
    row = lax.broadcasted_iota(jnp.int32, (rows, lanes), 0)
    lane = lax.broadcasted_iota(jnp.int32, (rows, lanes), 1)
    for z in range(depth):
        coef = [coef_ref[d, z].astype(jnp.float32) for d in range(6)]
        rhs = []
        for f in range(2):
            here = rock_ref[f, z]
            down = below_ref[f, :rows] if z == 0 else rock_ref[f, z - 1]
            up = above_ref[f, :rows] if z == depth - 1 else rock_ref[f, z + 1]
            west = jnp.where(row == 0, left_ref[f, z][None, :], pltpu.roll(here, 1, 0))
            east = jnp.where(row == rows - 1, right_ref[f, z][None, :], pltpu.roll(here, rows - 1, 0))
            south = jnp.where(lane == 0, 0.0, pltpu.roll(here, 1, 1))
            north = jnp.where(lane == lanes - 1, 0.0, pltpu.roll(here, lanes - 1, 1))
            total = coef[0] * down + coef[1] * up + coef[2] * west + coef[3] * east
            total = total + coef[4] * south + coef[5] * north
            leak = jnp.concatenate([leak_ref[f, z, j] for j in range(tiles)], axis=1)
            rhs.append(source_ref[f, z] + total + leak)
        inv = [inv_ref[i, z].astype(jnp.float32) for i in range(4)]
        for f in range(2):
            value = inv[2 * f] * rhs[0] + inv[2 * f + 1] * rhs[1]
            out_ref[f, z] = value
            high = value.astype(jnp.bfloat16)
            low = (value - high.astype(jnp.float32)).astype(jnp.bfloat16)
            for j in range(tiles):
                table_ref[f, z, j] = high[:, j * 128 : (j + 1) * 128]
                table_ref[fields + f, z, j] = low[:, j * 128 : (j + 1) * 128]
            first_ref[f, z] = value[0]
            last_ref[f, z] = value[rows - 1]
            if z == 0:
                low_ref[f, :rows] = value
                low_ref[f, rows:] = fracture_ref[f]
            if z == depth - 1:
                high_ref[f, :rows] = value
                high_ref[f, rows:] = fracture_ref[f]


def rock_step(rock, source, leak, below, above, left, right, coef, inverse, fracture):
    fields, depth, rows, lanes = rock.shape
    halo_rows = rows + fracture.shape[1]
    vmem = pl.BlockSpec(memory_space=pltpu.VMEM)
    return pl.pallas_call(
        rock_kernel,
        out_shape=(
            jax.ShapeDtypeStruct(rock.shape, jnp.float32),
            jax.ShapeDtypeStruct((fields, halo_rows, lanes), jnp.float32),
            jax.ShapeDtypeStruct((fields, halo_rows, lanes), jnp.float32),
            jax.ShapeDtypeStruct((fields, depth, lanes), jnp.float32),
            jax.ShapeDtypeStruct((fields, depth, lanes), jnp.float32),
            jax.ShapeDtypeStruct((2 * fields,) + leak.shape[1:], jnp.bfloat16),
        ),
        in_specs=[vmem] * 10,
        out_specs=(vmem,) * 6,
        cost_estimate=pl.CostEstimate(
            flops=40 * rock.size, transcendentals=0, bytes_accessed=20 * rock.size
        ),
        interpret=INTERPRET,
    )(rock, source, leak, below, above, left, right, coef, inverse, fracture)


def shards(
    rock_state,
    rock_source,
    transmissibility,
    cell_inverse,
    fracture_state,
    fracture_source,
    fracture_coupling,
    fracture_inverse,
    fracture_neighbours,
    contact_cell,
    contact_segment,
    contact_weight,
    contact_count,
):
    plane_count = lax.axis_size("plane")
    slab_count = lax.axis_size("slab")
    blocks = fracture_coupling.shape[0]
    segment_width = fracture_coupling.shape[-1]
    cell_table = contact_cell[0]
    slot_shape = cell_table.shape
    slot_index = lax.broadcasted_iota(jnp.int32, slot_shape, 1)
    slot_weight = jnp.where(slot_index < contact_count[0][:, None], contact_weight[0], 0.0)
    slot_weight_flat = slot_weight.reshape(-1)
    arrived_segment = lax.all_to_all(
        contact_segment[0], "slab", split_axis=0, concat_axis=0, tiled=True
    )
    my_part = lax.axis_index("slab") * plane_count + lax.axis_index("plane")
    owner_part = fracture_neighbours // blocks
    position = ((owner_part - my_part) // plane_count + 1) * blocks + fracture_neighbours % blocks
    rim_onehot = (
        position[:, :, None] == lax.broadcasted_iota(jnp.int32, (1, 1, 3 * blocks), 2)
    ).astype(jnp.bfloat16)
    cell_total = rock_state[0].size
    cell_rows = cell_total // 128
    cell_flat = cell_table.reshape(-1)
    _, depth, rows, lanes = rock_state.shape
    tiles = lanes // 128
    cell_z = cell_flat // (rows * lanes)
    cell_x = (cell_flat // lanes) % rows
    cell_y = cell_flat % lanes
    cell_row = (cell_z * tiles + cell_y // 128) * rows + cell_x
    cell_row_onehot = (
        cell_row[None, :] == lax.broadcasted_iota(jnp.int32, (cell_rows, 1), 0)
    ).astype(jnp.bfloat16)
    cell_col_mask = (
        (cell_y % 128)[:, None] == lax.broadcasted_iota(jnp.int32, (1, 128), 1)
    ).astype(jnp.bfloat16)
    segment_flat = arrived_segment.reshape(-1)
    segment_row_onehot = (
        (segment_flat // segment_width)[None, :] == lax.broadcasted_iota(jnp.int32, (blocks, 1), 0)
    ).astype(jnp.bfloat16)
    segment_col_mask = (
        (segment_flat % segment_width)[:, None]
        == lax.broadcasted_iota(jnp.int32, (1, segment_width), 1)
    ).astype(jnp.bfloat16)
    coef_z = transmissibility[0]
    coef_x = transmissibility[1]
    coef_y = transmissibility[2]
    forward_slab = [(i, i + 1) for i in range(slab_count - 1)]
    backward_slab = [(i + 1, i) for i in range(slab_count - 1)]
    forward_plane = [(i, i + 1) for i in range(plane_count - 1)]
    backward_plane = [(i + 1, i) for i in range(plane_count - 1)]
    rock_now = rock_state
    rock_table = rock_state.reshape(2, depth, rows, tiles, 128).transpose(0, 1, 3, 2, 4)
    rock_table = rock_table.reshape(2, cell_rows, 128)
    rock_high_part, rock_low_part = split_bf16(rock_table)
    rock_parts = jnp.concatenate([rock_high_part, rock_low_part], 0)
    fracture_start = fracture_state.astype(jnp.bfloat16).astype(jnp.float32)
    fracture_start = fracture_start.reshape(2, -1, rock_state.shape[-1])
    rock_low = jnp.concatenate([rock_now[:, 0], fracture_start], 1)
    rock_high = jnp.concatenate([rock_now[:, -1], fracture_start], 1)
    rock_first, rock_last = rock_now[:, :, 0], rock_now[:, :, -1]
    fracture_now = fracture_state
    source_blocks = fracture_source.reshape(2, blocks, segment_width)
    layer_rows = rock_now.shape[2]
    for sweep_index in range(ITERS):
        rock_picked = pick_parts(cell_row_onehot, cell_col_mask, rock_parts)
        send_rock = slot_weight_flat[None] * rock_picked
        fracture_table = fracture_now.reshape(2, blocks, segment_width)
        send_fracture = pick_values(segment_row_onehot, segment_col_mask, fracture_table)
        send = jnp.concatenate([send_rock, send_fracture], 0).reshape((4,) + slot_shape)
        got = lax.all_to_all(
            send.transpose(1, 0, 2), "slab", split_axis=0, concat_axis=0, tiled=True
        ).transpose(1, 0, 2)
        got_rock = got[:2].reshape(2, -1)
        got_fracture = got[2:].reshape(2, -1)
        fracture_low = fracture_now.astype(jnp.bfloat16).reshape(2, blocks, segment_width)
        fracture_wide = fracture_low.astype(jnp.float32).reshape(2, -1, rock_now.shape[-1])
        from_below = lax.ppermute(rock_high, "slab", forward_slab)
        from_above = lax.ppermute(rock_low, "slab", backward_slab)
        from_left = lax.ppermute(rock_last, "plane", forward_plane)
        from_right = lax.ppermute(rock_first, "plane", backward_plane)
        if sweep_index == 0:
            layer_above = shifted(transmissibility[0, :1], "slab", -1)
            layer_beside = shifted(transmissibility[1, :, :1], "plane", -1)
            upper_z = jnp.concatenate([coef_z[1:], layer_above], 0)
            upper_x = jnp.concatenate([coef_x[:, 1:], layer_beside], 1)
            upper_y = jnp.pad(coef_y[..., 1:], ((0, 0), (0, 0), (0, 1)))
            coef_all = jnp.stack([coef_z, upper_z, coef_x, upper_x, coef_y, upper_y])
        fracture_prev = from_below[:, layer_rows:].reshape(fracture_low.shape).astype(jnp.bfloat16)
        fracture_next_part = from_above[:, layer_rows:].reshape(
            fracture_low.shape
        ).astype(jnp.bfloat16)
        fracture_padded = jnp.concatenate([fracture_prev, fracture_low, fracture_next_part], 1)
        gathered = jnp.einsum(
            "bkq,fqj->fbkj", rim_onehot, fracture_padded, preferred_element_type=jnp.float32
        ).astype(jnp.bfloat16)
        coupled = jnp.einsum(
            "bkij,fbkj->fbi", fracture_coupling, gathered, preferred_element_type=jnp.float32
        )
        fracture_part = lax.optimization_barrier(source_blocks - coupled)
        leak_fracture = place_values(segment_row_onehot, segment_col_mask, got_rock)
        leak_rock = place_values(
            cell_row_onehot, cell_col_mask, slot_weight_flat[None] * got_fracture
        ).reshape(2, depth, tiles, rows, 128)
        fracture_rhs = (fracture_part + leak_fracture).astype(jnp.bfloat16)
        fracture_next = jnp.einsum(
            "bij,fbj->fbi", fracture_inverse, fracture_rhs, preferred_element_type=jnp.float32
        ).reshape(2, -1)
        rock_now, rock_low, rock_high, rock_first, rock_last, rock_table = rock_step(
            rock_now,
            rock_source,
            leak_rock,
            from_below,
            from_above,
            from_left,
            from_right,
            coef_all,
            cell_inverse,
            fracture_next.astype(jnp.bfloat16).astype(jnp.float32).reshape(fracture_wide.shape),
        )
        rock_parts = rock_table.reshape(4, cell_rows, 128)
        fracture_now = fracture_next
    return (rock_now, fracture_now)


def solution(mesh):
    return jax.shard_map(
        shards,
        mesh=mesh,
        in_specs=(
            P(None, "slab", "plane", None),
            P(None, "slab", "plane", None),
            P(None, "slab", "plane", None),
            P(None, "slab", "plane", None),
            P(None, ("slab", "plane")),
            P(None, ("slab", "plane")),
            P(("slab", "plane"), None, None, None),
            P(("slab", "plane"), None, None),
            P(("slab", "plane"), None),
            P("slab", "plane", None),
            P("slab", "plane", None),
            P("slab", "plane", None),
            P("slab", "plane"),
        ),
        out_specs=(P(None, "slab", "plane", None), P(None, ("slab", "plane"))),
        check_vma=False,
    )
```

```python
import jax
import jax.numpy as jnp
from jax import lax
from jax.sharding import PartitionSpec as P

from jax.experimental import pallas as pl
from jax.experimental.pallas import tpu as pltpu


ITERS = 3
INTERPRET = False


def shifted(value, axis, steps):
    count = lax.axis_size(axis)
    first, last = (max(0, -steps), min(count, count - steps))
    return lax.ppermute(value, axis, [(source, source + steps) for source in range(first, last)])


def split_bf16(value):
    high = lax.reduce_precision(value, exponent_bits=8, mantissa_bits=7)
    return high.astype(jnp.bfloat16), (value - high).astype(jnp.bfloat16)


def pick_values(row_onehot, col_mask, table):
    high, low = split_bf16(table)
    return pick_parts(row_onehot, col_mask, jnp.concatenate([high, low], 0))


def pick_joined(row_onehot, col_mask, parts):
    by_row = jnp.einsum("kc,frc->frk", col_mask, parts, preferred_element_type=jnp.float32)
    return jnp.sum(by_row * row_onehot.astype(jnp.float32)[None], axis=1)


def pick_parts(row_onehot, col_mask, parts):
    fields = parts.shape[0] // 2
    by_row = jnp.einsum("kc,grc->grk", col_mask, parts, preferred_element_type=jnp.float32)
    picked = jnp.sum(by_row * row_onehot.astype(jnp.float32)[None], axis=1)
    return picked[:fields] + picked[fields:]


def place_values(row_onehot, col_mask, values):
    fields = values.shape[0]
    high, low = split_bf16(values)
    parts = jnp.concatenate([high, low], 0)
    spread = parts[:, None, :] * row_onehot[None]
    placed = jnp.einsum("grk,kc->grc", spread, col_mask, preferred_element_type=jnp.float32)
    return placed[:fields] + placed[fields:]


def rock_kernel(
    rock_ref, source_ref, leak_ref, below_ref, above_ref, left_ref, right_ref, coef_ref, inv_ref,
    fracture_ref, out_ref, low_ref, high_ref, first_ref, last_ref, table_ref,
):
    _, depth, rows, lanes = rock_ref.shape
    tiles = leak_ref.shape[2]
    row = lax.broadcasted_iota(jnp.int32, (rows, lanes), 0)
    lane = lax.broadcasted_iota(jnp.int32, (rows, lanes), 1)
    for z in range(depth):
        coef = [coef_ref[d, z].astype(jnp.float32) for d in range(6)]
        rhs = []
        for f in range(2):
            here = rock_ref[f, z]
            down = below_ref[f, :rows] if z == 0 else rock_ref[f, z - 1]
            up = above_ref[f, :rows] if z == depth - 1 else rock_ref[f, z + 1]
            west = jnp.where(row == 0, left_ref[f, z][None, :], pltpu.roll(here, 1, 0))
            east = jnp.where(row == rows - 1, right_ref[f, z][None, :], pltpu.roll(here, rows - 1, 0))
            south = jnp.where(lane == 0, 0.0, pltpu.roll(here, 1, 1))
            north = jnp.where(lane == lanes - 1, 0.0, pltpu.roll(here, lanes - 1, 1))
            total = coef[0] * down + coef[1] * up + coef[2] * west + coef[3] * east
            total = total + coef[4] * south + coef[5] * north
            leak = jnp.concatenate([leak_ref[f, z, j] for j in range(tiles)], axis=1)
            rhs.append(source_ref[f, z] + total + leak)
        inv = [inv_ref[i, z].astype(jnp.float32) for i in range(4)]
        for f in range(2):
            value = inv[2 * f] * rhs[0] + inv[2 * f + 1] * rhs[1]
            out_ref[f, z] = value
            high = value.astype(jnp.bfloat16)
            low = (value - high.astype(jnp.float32)).astype(jnp.bfloat16)
            for j in range(tiles):
                table_ref[f, z, j, :, :128] = high[:, j * 128 : (j + 1) * 128]
                table_ref[f, z, j, :, 128:] = low[:, j * 128 : (j + 1) * 128]
            first_ref[f, z] = value[0]
            last_ref[f, z] = value[rows - 1]
            if z == 0:
                low_ref[f, :rows] = value
                low_ref[f, rows:] = fracture_ref[f]
            if z == depth - 1:
                high_ref[f, :rows] = value
                high_ref[f, rows:] = fracture_ref[f]


def rock_step(rock, source, leak, below, above, left, right, coef, inverse, fracture):
    fields, depth, rows, lanes = rock.shape
    halo_rows = rows + fracture.shape[1]
    vmem = pl.BlockSpec(memory_space=pltpu.VMEM)
    return pl.pallas_call(
        rock_kernel,
        out_shape=(
            jax.ShapeDtypeStruct(rock.shape, jnp.float32),
            jax.ShapeDtypeStruct((fields, halo_rows, lanes), jnp.float32),
            jax.ShapeDtypeStruct((fields, halo_rows, lanes), jnp.float32),
            jax.ShapeDtypeStruct((fields, depth, lanes), jnp.float32),
            jax.ShapeDtypeStruct((fields, depth, lanes), jnp.float32),
            jax.ShapeDtypeStruct(leak.shape[:-1] + (2 * leak.shape[-1],), jnp.bfloat16),
        ),
        in_specs=[vmem] * 10,
        out_specs=(vmem,) * 6,
        cost_estimate=pl.CostEstimate(
            flops=40 * rock.size, transcendentals=0, bytes_accessed=20 * rock.size
        ),
        interpret=INTERPRET,
    )(rock, source, leak, below, above, left, right, coef, inverse, fracture)


def shards(
    rock_state,
    rock_source,
    transmissibility,
    cell_inverse,
    fracture_state,
    fracture_source,
    fracture_coupling,
    fracture_inverse,
    fracture_neighbours,
    contact_cell,
    contact_segment,
    contact_weight,
    contact_count,
):
    plane_count = lax.axis_size("plane")
    slab_count = lax.axis_size("slab")
    blocks = fracture_coupling.shape[0]
    segment_width = fracture_coupling.shape[-1]
    cell_table = contact_cell[0]
    slot_shape = cell_table.shape
    slot_index = lax.broadcasted_iota(jnp.int32, slot_shape, 1)
    slot_weight = jnp.where(slot_index < contact_count[0][:, None], contact_weight[0], 0.0)
    slot_weight_flat = slot_weight.reshape(-1)
    arrived_segment = lax.all_to_all(
        contact_segment[0], "slab", split_axis=0, concat_axis=0, tiled=True
    )
    my_part = lax.axis_index("slab") * plane_count + lax.axis_index("plane")
    owner_part = fracture_neighbours // blocks
    position = ((owner_part - my_part) // plane_count + 1) * blocks + fracture_neighbours % blocks
    rim_onehot = (
        position[:, :, None] == lax.broadcasted_iota(jnp.int32, (1, 1, 3 * blocks), 2)
    ).astype(jnp.bfloat16)
    cell_total = rock_state[0].size
    cell_rows = cell_total // 128
    cell_flat = cell_table.reshape(-1)
    _, depth, rows, lanes = rock_state.shape
    tiles = lanes // 128
    cell_z = cell_flat // (rows * lanes)
    cell_x = (cell_flat // lanes) % rows
    cell_y = cell_flat % lanes
    cell_row = (cell_z * tiles + cell_y // 128) * rows + cell_x
    cell_row_onehot = (
        cell_row[None, :] == lax.broadcasted_iota(jnp.int32, (cell_rows, 1), 0)
    ).astype(jnp.bfloat16)
    cell_col_mask = (
        (cell_y % 128)[:, None] == lax.broadcasted_iota(jnp.int32, (1, 128), 1)
    ).astype(jnp.bfloat16)
    segment_flat = arrived_segment.reshape(-1)
    segment_row_onehot = (
        (segment_flat // segment_width)[None, :] == lax.broadcasted_iota(jnp.int32, (blocks, 1), 0)
    ).astype(jnp.bfloat16)
    segment_col_mask = (
        (segment_flat % segment_width)[:, None]
        == lax.broadcasted_iota(jnp.int32, (1, segment_width), 1)
    ).astype(jnp.bfloat16)
    coef_z = transmissibility[0]
    coef_x = transmissibility[1]
    coef_y = transmissibility[2]
    forward_slab = [(i, i + 1) for i in range(slab_count - 1)]
    backward_slab = [(i + 1, i) for i in range(slab_count - 1)]
    forward_plane = [(i, i + 1) for i in range(plane_count - 1)]
    backward_plane = [(i + 1, i) for i in range(plane_count - 1)]
    rock_now = rock_state
    rock_table = rock_state.reshape(2, depth, rows, tiles, 128).transpose(0, 1, 3, 2, 4)
    rock_table = rock_table.reshape(2, cell_rows, 128)
    rock_high_part, rock_low_part = split_bf16(rock_table)
    rock_parts = jnp.concatenate([rock_high_part, rock_low_part], 2)
    cell_col_pair = jnp.concatenate([cell_col_mask, cell_col_mask], 1)
    fracture_start = fracture_state.astype(jnp.bfloat16).astype(jnp.float32)
    fracture_start = fracture_start.reshape(2, -1, rock_state.shape[-1])
    rock_low = jnp.concatenate([rock_now[:, 0], fracture_start], 1)
    rock_high = jnp.concatenate([rock_now[:, -1], fracture_start], 1)
    rock_first, rock_last = rock_now[:, :, 0], rock_now[:, :, -1]
    fracture_now = fracture_state
    source_blocks = fracture_source.reshape(2, blocks, segment_width)
    layer_rows = rock_now.shape[2]
    for sweep_index in range(ITERS):
        rock_picked = pick_joined(cell_row_onehot, cell_col_pair, rock_parts)
        send_rock = slot_weight_flat[None] * rock_picked
        fracture_table = fracture_now.reshape(2, blocks, segment_width)
        send_fracture = pick_values(segment_row_onehot, segment_col_mask, fracture_table)
        send = jnp.concatenate([send_rock, send_fracture], 0).reshape((4,) + slot_shape)
        got = lax.all_to_all(
            send.transpose(1, 0, 2), "slab", split_axis=0, concat_axis=0, tiled=True
        ).transpose(1, 0, 2)
        got_rock = got[:2].reshape(2, -1)
        got_fracture = got[2:].reshape(2, -1)
        fracture_low = fracture_now.astype(jnp.bfloat16).reshape(2, blocks, segment_width)
        fracture_wide = fracture_low.astype(jnp.float32).reshape(2, -1, rock_now.shape[-1])
        from_below = lax.ppermute(rock_high, "slab", forward_slab)
        from_above = lax.ppermute(rock_low, "slab", backward_slab)
        from_left = lax.ppermute(rock_last, "plane", forward_plane)
        from_right = lax.ppermute(rock_first, "plane", backward_plane)
        if sweep_index == 0:
            layer_above = shifted(transmissibility[0, :1], "slab", -1)
            layer_beside = shifted(transmissibility[1, :, :1], "plane", -1)
            upper_z = jnp.concatenate([coef_z[1:], layer_above], 0)
            upper_x = jnp.concatenate([coef_x[:, 1:], layer_beside], 1)
            upper_y = jnp.pad(coef_y[..., 1:], ((0, 0), (0, 0), (0, 1)))
            coef_all = jnp.stack([coef_z, upper_z, coef_x, upper_x, coef_y, upper_y])
        fracture_prev = from_below[:, layer_rows:].reshape(fracture_low.shape).astype(jnp.bfloat16)
        fracture_next_part = from_above[:, layer_rows:].reshape(
            fracture_low.shape
        ).astype(jnp.bfloat16)
        fracture_padded = jnp.concatenate([fracture_prev, fracture_low, fracture_next_part], 1)
        gathered = jnp.einsum(
            "bkq,fqj->fbkj", rim_onehot, fracture_padded, preferred_element_type=jnp.float32
        ).astype(jnp.bfloat16)
        coupled = jnp.einsum(
            "bkij,fbkj->fbi", fracture_coupling, gathered, preferred_element_type=jnp.float32
        )
        fracture_part = lax.optimization_barrier(source_blocks - coupled)
        leak_fracture = place_values(segment_row_onehot, segment_col_mask, got_rock)
        leak_rock = place_values(
            cell_row_onehot, cell_col_mask, slot_weight_flat[None] * got_fracture
        ).reshape(2, depth, tiles, rows, 128)
        fracture_rhs = (fracture_part + leak_fracture).astype(jnp.bfloat16)
        fracture_next = jnp.einsum(
            "bij,fbj->fbi", fracture_inverse, fracture_rhs, preferred_element_type=jnp.float32
        ).reshape(2, -1)
        rock_now, rock_low, rock_high, rock_first, rock_last, rock_table = rock_step(
            rock_now,
            rock_source,
            leak_rock,
            from_below,
            from_above,
            from_left,
            from_right,
            coef_all,
            cell_inverse,
            fracture_next.astype(jnp.bfloat16).astype(jnp.float32).reshape(fracture_wide.shape),
        )
        rock_parts = rock_table.reshape(2, cell_rows, 256)
        fracture_now = fracture_next
    return (rock_now, fracture_now)


def solution(mesh):
    return jax.shard_map(
        shards,
        mesh=mesh,
        in_specs=(
            P(None, "slab", "plane", None),
            P(None, "slab", "plane", None),
            P(None, "slab", "plane", None),
            P(None, "slab", "plane", None),
            P(None, ("slab", "plane")),
            P(None, ("slab", "plane")),
            P(("slab", "plane"), None, None, None),
            P(("slab", "plane"), None, None),
            P(("slab", "plane"), None),
            P("slab", "plane", None),
            P("slab", "plane", None),
            P("slab", "plane", None),
            P("slab", "plane"),
        ),
        out_specs=(P(None, "slab", "plane", None), P(None, ("slab", "plane"))),
        check_vma=False,
    )
```
